32 devices in a mesh: req: 4 (over y, x), mp: 8 (over z, core).
Axes of the slice: x: 2, y: 2, z: 4, core: 2. Of those that a mesh axis runs over, the one named last changes fastest.
Arguments:
- tokens: bfloat16 [1024, 2048], P('req'), may hold values from -6 to 6
- lengths: int32 [4, 8], P('req'), may hold values from 1 to 80, 256 in all within a row
- response: int32 [1024], P('req'), may hold values 0 or 1
- targets: int32 [1024], replicated, may hold values from 0 to 32063, as said below
- attn_gain: float32 [2, 2048], replicated, may hold values from 0.5 to 1.5
- w_query: bfloat16 [2, 2048, 2048], P(None, None, 'mp')
- w_key: bfloat16 [2, 2048, 512], replicated, may hold values from -0.125 to 0.125
- w_value: bfloat16 [2, 2048, 512], replicated, may hold values from -0.125 to 0.125
- output_weight: bfloat16 [2, 2048, 2048], P(None, 'mp'), may hold values from -0.125 to 0.125
- mlp_gain: float32 [2, 2048], replicated, may hold values from 0.5 to 1.5
- w_gate: bfloat16 [2, 2048, 8192], P(None, None, 'mp'), may hold values from -0.125 to 0.125
- w_up: bfloat16 [2, 2048, 8192], P(None, None, 'mp'), may hold values from -0.125 to 0.125
- w_down: bfloat16 [2, 8192, 2048], P(None, 'mp'), may hold values from -0.0625 to 0.0625
- final_gain: float32 [2, 2048], replicated, may hold values from 0.5 to 1.5
- w_head: bfloat16 [2, 2048, 32064], P(None, None, ('req', 'mp'))
Outputs:
- token_diff: float32 [1024], P(('req', 'mp'))
- request_sum: float32 [4, 8], P('req')
- request_peak: float32 [4, 8], P('req')
The draws below stay inside these ranges and needn't reach their ends.
Inputs may be any that keep to these rules, and one draw needn't show every extreme that they name: `lengths`: each row sums to 256; some request of each tenant has exactly 80 tokens. `targets`: vocabulary ids.
All inputs are finite; a program needn't handle non-finite values. No bound on the sum of `response` on one device may be relied on, other than what follows from the above.
Results may differ from the reference program's by a relative error of at most 0.04.
Values may be sent and summed in bfloat16 or wider, within the bound.
No kernel may reach another device: no remote copies, remote signals or barrier semaphores. Data moves between devices by JAX's collectives and lax.ppermute only.
A program may use at most 128 MiB of HBM per device.

```python
import math
import jax
import jax.numpy as jnp
import numpy as np
from jax import lax

D = 2048
HEADS = 32
KV_HEADS = 8
HEAD_DIM = 64
FF = 8192
V_DEV = 1002
TOK_GRP = 256
RPT = 8
TENANTS = 4
TOKENS = 1024
V = 32064
MOST_LEN = 80
DEVICES = 32


def draw_targets(key, part):
    per_block = TOKENS // DEVICES
    row_ids = jnp.arange(TOKENS, dtype=jnp.int32)
    block_ids = row_ids // per_block
    inner_ids = row_ids % per_block
    mixed_ids = inner_ids + block_ids
    structured = mixed_ids % 2 == 0
    partner_table = jnp.array([1, DEVICES - 1, DEVICES // 2], dtype=jnp.int32)
    partner = partner_table[mixed_ids // 2 % 3]
    slice_fixed = (block_ids + partner) % DEVICES
    slice_random = jax.random.randint(jax.random.fold_in(key, 3), (TOKENS,), 0, DEVICES, dtype=jnp.int32)
    column = jax.random.randint(jax.random.fold_in(key, 5), (TOKENS,), 0, V_DEV, dtype=jnp.int32)
    chosen_slice = jnp.where(structured, slice_fixed, slice_random)
    picked = (chosen_slice * V_DEV + column).astype(jnp.int32)
    picked = jnp.where(row_ids == 0, jnp.int32(0), picked)
    picked = jnp.where(row_ids == TOKENS - 1, jnp.int32(V - 1), picked)
    return picked.astype(jnp.int32)


def draw_w_query(key, part):
    base_values = jax.random.normal(key, (2, D, HEADS * HEAD_DIM), jnp.float32)
    base_values = jnp.clip(base_values, -6.0, 6.0) / jnp.sqrt(jnp.float32(D))
    return base_values.astype(jnp.bfloat16)


def draw_w_head(key, part):
    base_values = jax.random.normal(key, (2, D, V), jnp.float32)
    base_values = jnp.clip(base_values, -6.0, 6.0) * (3.0 / jnp.sqrt(jnp.float32(D)))
    return base_values.astype(jnp.bfloat16)


def place_ends(values, rng, least, largest):
    longest = values.shape.index(max(values.shape))
    spots = []
    for shift in (0, 1):
        where = [jax.random.randint(jax.random.fold_in(rng, axis), (), 0, length) for axis, length in enumerate(values.shape)]
        where[longest] = (where[longest] + shift) % values.shape[longest]
        spots.append(tuple(where))
    return values.at[spots[0]].set(least).at[spots[1]].set(largest)


def steps_of(rng, shape, cuts, least, high):
    gain, own = 1.0, jax.random.fold_in(rng, 6)
    for dim, shards_of in cuts:
        draws = jnp.exp(jax.random.uniform(jax.random.fold_in(own, dim), (shards_of,), jnp.float32, least / len(cuts), high / len(cuts)))
        gain = gain * jnp.repeat(draws, shape[dim] // shards_of).reshape([-1 if axis == dim else 1 for axis in range(len(shape))])
    return gain


def profile(amount, total, most, slope):
    weights = [(1 << 20) // math.isqrt(rank ** slope) + 1 for rank in range(2, amount + 1)]
    spare, holding = total - most - (amount - 1), [1] * (amount - 1)
    while spare > 0:
        candidates = [i for i in range(amount - 1) if holding[i] < most]
        pool, left = sum([weights[i] for i in candidates]), spare
        for i in candidates:
            addition = min(most - holding[i], max(1, left * weights[i] // pool), spare)
            holding[i] = holding[i] + addition
            spare = spare - addition
    return np.array([most] + holding)


def ragged(stream_key, number_of, total, bound, lean):
    if number_of == 2:
        one = jax.random.randint(stream_key, (), max(1, total - bound), min(bound, total - 1) + 1)
        return jnp.stack([one, total - one])
    sizes = jnp.asarray(profile(number_of, total, bound, lean), jnp.int32)
    twos = (number_of - 1) // 2
    donor, receiver = sizes[1:1 + 2 * twos:2], sizes[2:2 + 2 * twos:2]
    room = jnp.minimum(donor - 1, bound - receiver)
    passed = jax.random.randint(jax.random.fold_in(stream_key, 1), (twos,), 0, 1 << 20) % (room + 1)
    sizes = sizes.at[1:1 + 2 * twos:2].set(donor - passed).at[2:2 + 2 * twos:2].set(receiver + passed)
    return sizes[jax.random.permutation(jax.random.fold_in(stream_key, 2), number_of)]


def normal_values(own_key, dims, deviation, most, split=(), kind=jnp.bfloat16):
    values = deviation * jax.random.normal(own_key, dims, jnp.float32)
    if split:
        values = values * steps_of(own_key, dims, split, -0.22, 0.18)
    return jnp.clip(values, -most, most).astype(kind)


def setup_inputs(seed: int = 0) -> dict:
    streams_of = jax.random.split(jax.random.key(seed), 16)
    tokens = normal_values(streams_of[0], (TOKENS, D), 1.0, 6.0, ((0, 4),))
    lengths = jax.vmap(lambda own: ragged(own, RPT, TOK_GRP, MOST_LEN, 2))(jax.random.split(streams_of[1], TENANTS)).reshape((TENANTS, RPT)).astype(jnp.int32)
    response = place_ends((jax.random.randint(streams_of[2], (TOKENS,), 0, 8) < 3).astype(jnp.int32), jax.random.fold_in(streams_of[2], 1), 0, 1)
    targets = draw_targets(jax.random.fold_in(streams_of[15], 71), 0)
    attn_gain = jnp.clip(1.0 + 0.1 * jax.random.normal(streams_of[4], (2, D), jnp.float32), 0.5, 1.5)
    w_query = draw_w_query(jax.random.fold_in(streams_of[15], 71), 0)
    w_key = normal_values(streams_of[6], (2, D, KV_HEADS * HEAD_DIM), D ** -0.5, 0.125)
    w_value = normal_values(streams_of[7], (2, D, KV_HEADS * HEAD_DIM), D ** -0.5, 0.125)
    output_weight = normal_values(streams_of[8], (2, HEADS * HEAD_DIM, D), (HEADS * HEAD_DIM) ** -0.5, 0.125, ((1, 8),))
    mlp_gain = jnp.clip(1.0 + 0.1 * jax.random.normal(streams_of[9], (2, D), jnp.float32), 0.5, 1.5)
    w_gate = normal_values(streams_of[10], (2, D, FF), D ** -0.5, 0.125, ((2, 8),))
    w_up = normal_values(streams_of[11], (2, D, FF), D ** -0.5, 0.125, ((2, 8),))
    w_down = normal_values(streams_of[12], (2, FF, D), FF ** -0.5, 0.0625, ((1, 8),))
    final_gain = jnp.clip(1.0 + 0.1 * jax.random.normal(streams_of[13], (2, D), jnp.float32), 0.5, 1.5)
    w_head = draw_w_head(jax.random.fold_in(streams_of[15], 71), 0)
    return dict(tokens=tokens, lengths=lengths, response=response, targets=targets, attn_gain=attn_gain, w_query=w_query, w_key=w_key, w_value=w_value, output_weight=output_weight, mlp_gain=mlp_gain, w_gate=w_gate, w_up=w_up, w_down=w_down, final_gain=final_gain, w_head=w_head)


epsilon = 1e-05
theta = 500000.0

def rms_scale(entries, scaling):
    entries = entries.astype(jnp.float32)
    inverse = lax.rsqrt(lax.optimization_barrier(jnp.mean(entries * entries, axis=-1, keepdims=True)) + epsilon)
    return entries * inverse * scaling.astype(jnp.float32)

def rotate(entries, positions):
    halfway = entries.shape[-1] // 2
    frequency = theta ** (-jnp.arange(halfway, dtype=jnp.float32) * 2.0 / entries.shape[-1])
    angles = positions.astype(jnp.float32)[:, None] * frequency[None, :]
    cosine = jnp.cos(angles)
    sine_part = jnp.sin(angles)
    former = entries[..., :halfway]
    latter = entries[..., halfway:]
    return jnp.concatenate([former * cosine - latter * sine_part, latter * cosine + former * sine_part], axis=-1)

def request_layout(length_row, slot_count):
    length_row = length_row.astype(jnp.int32)
    end_slot = jnp.cumsum(length_row, dtype=jnp.int32)
    start_slot = end_slot - length_row
    slot_ids = jnp.arange(slot_count, dtype=jnp.int32)
    member = (slot_ids[:, None] >= start_slot[None, :]) & (slot_ids[:, None] < end_slot[None, :])
    segment = lax.optimization_barrier(jnp.sum((slot_ids[:, None] >= end_slot[None, :]).astype(jnp.int32), axis=1))
    offset = lax.optimization_barrier(jnp.sum(jnp.where(member, start_slot[None, :], 0), axis=1)).astype(jnp.int32)
    return (member, segment, slot_ids - offset)

def allowed_pairs(segment):
    slot_ids = jnp.arange(segment.shape[0], dtype=jnp.int32)
    return (segment[:, None] == segment[None, :]) & (slot_ids[None, :] <= slot_ids[:, None])

def attend_heads(query, key_rows, value_rows, positions, allowed, repeat_times):
    slot_count = query.shape[0]
    query = rotate(query.reshape(slot_count, -1, HEAD_DIM).transpose(1, 0, 2), positions).astype(jnp.bfloat16)
    key_rows = rotate(key_rows.reshape(slot_count, -1, HEAD_DIM).transpose(1, 0, 2), positions).astype(jnp.bfloat16)
    value_rows = value_rows.reshape(slot_count, -1, HEAD_DIM).transpose(1, 0, 2).astype(jnp.bfloat16)
    key_rows = jnp.repeat(key_rows, repeat_times, axis=0)
    value_rows = jnp.repeat(value_rows, repeat_times, axis=0)
    scores = jnp.einsum('hqd,hkd->hqk', query.astype(jnp.float32), key_rows.astype(jnp.float32)) * HEAD_DIM ** (-0.5)
    scores = jnp.where(allowed[None], scores, -1e+30)
    highest = lax.optimization_barrier(jnp.max(scores, axis=-1, keepdims=True))
    weights = jnp.exp(scores - highest)
    probs = (weights / lax.optimization_barrier(jnp.sum(weights, axis=-1, keepdims=True))).astype(jnp.bfloat16)
    attended = jnp.einsum('hqk,hkd->hqd', probs.astype(jnp.float32), value_rows.astype(jnp.float32)).astype(jnp.bfloat16)
    return attended.transpose(1, 0, 2).reshape(slot_count, -1)

def reference(tokens, lengths, response, targets, attn_gain, w_query, w_key, w_value, output_weight, mlp_gain, w_gate, w_up, w_down, final_gain, w_head):
    finals = []
    members = []
    for tenant in range(TENANTS):
        tenant_rows = tokens[tenant * TOK_GRP:(tenant + 1) * TOK_GRP]
        member, segment, positions = request_layout(lengths[tenant], TOK_GRP)
        members.append(member.astype(jnp.float32))
        allowed = allowed_pairs(segment)
        per_model = []
        for model in range(2):
            normed = rms_scale(tenant_rows, attn_gain[model]).astype(jnp.bfloat16)
            query = jnp.dot(normed, w_query[model], preferred_element_type=jnp.float32)
            key_rows = jnp.dot(normed, w_key[model], preferred_element_type=jnp.float32)
            value_rows = jnp.dot(normed, w_value[model], preferred_element_type=jnp.float32)
            attended = attend_heads(query, key_rows, value_rows, positions, allowed, HEADS // KV_HEADS)
            residual = tenant_rows.astype(jnp.float32) + jnp.dot(attended, output_weight[model], preferred_element_type=jnp.float32)
            normed_mid = rms_scale(residual, mlp_gain[model]).astype(jnp.bfloat16)
            gate_part = jnp.dot(normed_mid, w_gate[model], preferred_element_type=jnp.float32)
            lift_part = jnp.dot(normed_mid, w_up[model], preferred_element_type=jnp.float32)
            hidden = (jax.nn.silu(gate_part) * lift_part).astype(jnp.bfloat16)
            final = residual + jnp.dot(hidden, w_down[model], preferred_element_type=jnp.float32)
            per_model.append(rms_scale(final, final_gain[model]).astype(jnp.bfloat16))
        finals.append(jnp.stack(per_model))
    finals = jnp.concatenate(finals, axis=1)
    block_rows = 32
    block_count = TOKENS // block_rows
    shaped = finals.reshape(2, block_count, block_rows, D).transpose(1, 0, 2, 3)
    wanted = targets.reshape(block_count, block_rows).astype(jnp.int32)

    def score_block(item):
        row_block, picks = item
        results = []
        for model in range(2):
            logits = jnp.dot(row_block[model], w_head[model], preferred_element_type=jnp.float32)
            highest = lax.optimization_barrier(jnp.max(logits, axis=-1, keepdims=True))
            normalizer = highest[:, 0] + jnp.log(lax.optimization_barrier(jnp.sum(jnp.exp(logits - highest), axis=-1)))
            chosen_token = jnp.take_along_axis(logits, picks[:, None], axis=1)[:, 0]
            results.append(chosen_token - normalizer)
        return jnp.stack(results)
    log_likelihood = lax.map(score_block, (shaped, wanted))
    log_likelihood = log_likelihood.transpose(1, 0, 2).reshape(2, TOKENS)
    token_diff = (log_likelihood[0] - log_likelihood[1]) * response.astype(jnp.float32)
    sums = []
    peaks = []
    for tenant in range(TENANTS):
        tenant_difference = token_diff[tenant * TOK_GRP:(tenant + 1) * TOK_GRP]
        sums.append(jnp.dot(tenant_difference, members[tenant], precision=lax.Precision.HIGHEST))
        peaks.append(lax.optimization_barrier(jnp.max(members[tenant] * jnp.abs(tenant_difference)[:, None], axis=0)))
    return (token_diff, jnp.stack(sums), jnp.stack(peaks))
```

```python
import jax
import jax.numpy as jnp
from jax import lax
from jax.sharding import PartitionSpec as P

HEADS = 32
KV_HEADS = 8
HEAD_DIM = 64


epsilon = 1e-05
theta = 500000.0


def merged(part, axis, combine):
    gathered = jax.tree.map(lambda a: lax.all_gather(a, axis), part)

    def take(source):
        return jax.tree.map(lambda a: lax.dynamic_index_in_dim(a, source, 0, False), gathered)

    return lax.fori_loop(
        1, lax.axis_size(axis), lambda source, state: combine(state, take(source)), take(0)
    )


def rms_scale(entries, scaling):
    entries = entries.astype(jnp.float32)
    inverse = lax.rsqrt(jnp.mean(entries * entries, axis=-1, keepdims=True) + epsilon)
    return entries * inverse * scaling


def rotate(entries, positions):
    halfway = entries.shape[-1] // 2
    frequency = theta ** (-jnp.arange(halfway, dtype=jnp.float32) * 2.0 / entries.shape[-1])
    angles = positions.astype(jnp.float32)[:, None] * frequency[None, :]
    cosine = jnp.cos(angles)
    sine_part = jnp.sin(angles)
    former = entries[..., :halfway]
    latter = entries[..., halfway:]
    return jnp.concatenate(
        [former * cosine - latter * sine_part, latter * cosine + former * sine_part], axis=-1
    )


def request_layout(length_row, slot_count):
    end_slot = jnp.cumsum(length_row, dtype=jnp.int32)
    start_slot = end_slot - length_row
    slot_ids = jnp.arange(slot_count, dtype=jnp.int32)
    member = (slot_ids[:, None] >= start_slot[None, :]) & (slot_ids[:, None] < end_slot[None, :])
    segment = jnp.sum((slot_ids[:, None] >= end_slot[None, :]).astype(jnp.int32), axis=1)
    offset = jnp.sum(jnp.where(member, start_slot[None, :], 0), axis=1)
    return (member, segment, slot_ids - offset)


def allowed_pairs(segment):
    slot_ids = jnp.arange(segment.shape[0], dtype=jnp.int32)
    return (segment[:, None] == segment[None, :]) & (slot_ids[None, :] <= slot_ids[:, None])


def attend_heads(query, key_rows, value_rows, positions, allowed, repeat_times):
    slot_count = query.shape[0]
    query = rotate(query.reshape(slot_count, -1, HEAD_DIM).transpose(1, 0, 2), positions).astype(
        jnp.bfloat16
    )
    key_rows = rotate(
        key_rows.reshape(slot_count, -1, HEAD_DIM).transpose(1, 0, 2), positions
    ).astype(jnp.bfloat16)
    value_rows = (
        value_rows.reshape(slot_count, -1, HEAD_DIM).transpose(1, 0, 2).astype(jnp.bfloat16)
    )
    key_rows = jnp.repeat(key_rows, repeat_times, axis=0)
    value_rows = jnp.repeat(value_rows, repeat_times, axis=0)
    scores = jnp.einsum(
        "hqd,hkd->hqk", query.astype(jnp.float32), key_rows.astype(jnp.float32)
    ) * HEAD_DIM ** (-0.5)
    scores = jnp.where(allowed[None], scores, -1e30)
    highest = jnp.max(scores, axis=-1, keepdims=True)
    weights = jnp.exp(scores - highest)
    probs = (weights / jnp.sum(weights, axis=-1, keepdims=True)).astype(jnp.bfloat16)
    attended = jnp.einsum(
        "hqk,hkd->hqd", probs.astype(jnp.float32), value_rows.astype(jnp.float32)
    ).astype(jnp.bfloat16)
    return attended.transpose(1, 0, 2).reshape(slot_count, -1)


def per_device(
    tokens,
    lengths,
    response,
    targets,
    attn_gain,
    w_query,
    w_key,
    w_value,
    output_weight,
    mlp_gain,
    w_gate,
    w_up,
    w_down,
    final_gain,
    w_head,
):
    group_rows = tokens.shape[0]
    own_rows = group_rows // lax.axis_size("mp")
    mp_index = lax.axis_index("mp")
    member, segment, positions = request_layout(lengths[0], group_rows)
    allowed = allowed_pairs(segment)
    heads_here = w_query.shape[2] // HEAD_DIM
    sharing = HEADS // KV_HEADS
    kv_here = max(1, heads_here // sharing)
    kv_first = mp_index * heads_here // sharing * HEAD_DIM
    key_cols = lax.dynamic_slice_in_dim(w_key, kv_first, kv_here * HEAD_DIM, 2)
    value_columns = lax.dynamic_slice_in_dim(w_value, kv_first, kv_here * HEAD_DIM, 2)
    attended_list = []
    for model in range(2):
        normed = rms_scale(tokens, attn_gain[model]).astype(jnp.bfloat16)
        query = jnp.dot(normed, w_query[model], preferred_element_type=jnp.float32)
        keys_here = jnp.dot(normed, key_cols[model], preferred_element_type=jnp.float32)
        values_here = jnp.dot(normed, value_columns[model], preferred_element_type=jnp.float32)
        attended_list.append(
            attend_heads(
                query, keys_here, values_here, positions, allowed, min(sharing, heads_here)
            )
        )
    attended = jnp.stack(attended_list, axis=1)
    selected_rows = attended
    mixed = lax.psum_scatter(
        jnp.einsum(
            "kbq,bqo->kbo", selected_rows, output_weight, preferred_element_type=jnp.float32
        ),
        "mp",
        scatter_dimension=0,
        tiled=True,
    )
    own_tokens = lax.dynamic_slice_in_dim(tokens, mp_index * own_rows, own_rows, 0)
    residual = own_tokens.astype(jnp.float32)[:, None, :] + mixed
    normed_mid = rms_scale(residual, mlp_gain).astype(jnp.bfloat16)
    row_block = lax.all_gather(normed_mid, "mp", axis=0, tiled=True)
    gate_part = jnp.einsum("nmd,mdf->nmf", row_block, w_gate, preferred_element_type=jnp.float32)
    lift_part = jnp.einsum("nmd,mdf->nmf", row_block, w_up, preferred_element_type=jnp.float32)
    hidden = (jax.nn.silu(gate_part) * lift_part).astype(jnp.bfloat16)
    selected_rows = hidden
    final = residual + lax.psum_scatter(
        jnp.einsum("nmf,mfd->nmd", selected_rows, w_down, preferred_element_type=jnp.float32),
        "mp",
        scatter_dimension=0,
        tiled=True,
    )
    closing = rms_scale(final, final_gain).astype(jnp.bfloat16)
    vocab_here = w_head.shape[2]
    vocab_first = lax.axis_index(("req", "mp")) * vocab_here
    column_ids = jnp.arange(vocab_here, dtype=jnp.int32)
    logits = jnp.einsum(
        "nmd,mdv->mnv",
        lax.all_gather(closing, ("req", "mp"), axis=0, tiled=True),
        w_head,
        preferred_element_type=jnp.float32,
    )
    peak_part = jnp.max(logits, axis=-1)
    total_part = jnp.sum(jnp.exp(logits - peak_part[..., None]), axis=-1)
    wanted = targets - vocab_first
    hit_part = jnp.sum(
        jnp.where(column_ids[None, None, :] == wanted[None, :, None], logits, 0.0), axis=-1
    )

    groups = lax.axis_size("req")
    parts = lax.axis_size("mp")
    stats = jnp.stack([peak_part, total_part, hit_part])
    tenant_stats = stats.reshape(3, 2, groups, group_rows).transpose(2, 0, 1, 3)
    outgoing = jnp.broadcast_to(
        tenant_stats[:, None], (groups, parts, 3, 2, group_rows)
    ).reshape(groups * parts, 3, 2, group_rows)
    incoming = lax.all_to_all(outgoing, ("req", "mp"), 0, 0, tiled=True)
    peak_all = jnp.max(incoming[:, 0], axis=0)
    total_all = jnp.sum(incoming[:, 1] * jnp.exp(incoming[:, 0] - peak_all[None]), axis=0)
    hit_all = jnp.sum(incoming[:, 2], axis=0)
    log_likelihood = hit_all - (peak_all + jnp.log(total_all))
    gap = log_likelihood[0] - log_likelihood[1]
    group_gap = gap * response.astype(jnp.float32)
    token_out = lax.dynamic_slice_in_dim(group_gap, mp_index * own_rows, own_rows, 0)
    member_weights = member.astype(jnp.float32)
    request_sum = jnp.dot(group_gap, member_weights, precision=lax.Precision.HIGHEST)
    request_peak = jnp.max(member_weights * jnp.abs(group_gap)[:, None], axis=0)
    return (token_out, request_sum[None, :], request_peak[None, :])


def solution(mesh):
    placed = (
        P("req", None),
        P("req", None),
        P("req"),
        P(),
        P(),
        P(None, None, "mp"),
        P(),
        P(),
        P(None, "mp", None),
        P(),
        P(None, None, "mp"),
        P(None, None, "mp"),
        P(None, "mp", None),
        P(),
        P(None, None, ("req", "mp")),
    )
    return jax.shard_map(
        per_device,
        mesh=mesh,
        in_specs=placed,
        out_specs=(P(("req", "mp")), P("req", None), P("req", None)),
        check_vma=False,
    )
```

```python
import jax
import jax.numpy as jnp
from jax import lax
from jax.sharding import PartitionSpec as P

HEADS = 32
KV_HEADS = 8
HEAD_DIM = 64


epsilon = 1e-05
theta = 500000.0


def merged(part, axis, combine):
    gathered = jax.tree.map(lambda a: lax.all_gather(a, axis), part)

    def take(source):
        return jax.tree.map(lambda a: lax.dynamic_index_in_dim(a, source, 0, False), gathered)

    return lax.fori_loop(
        1, lax.axis_size(axis), lambda source, state: combine(state, take(source)), take(0)
    )


def rms_scale(entries, scaling):
    entries = entries.astype(jnp.float32)
    inverse = lax.rsqrt(jnp.mean(entries * entries, axis=-1, keepdims=True) + epsilon)
    return entries * inverse * scaling


def rotate(entries, positions):
    halfway = entries.shape[-1] // 2
    frequency = theta ** (-jnp.arange(halfway, dtype=jnp.float32) * 2.0 / entries.shape[-1])
    angles = positions.astype(jnp.float32)[:, None] * frequency[None, :]
    cosine = jnp.cos(angles)
    sine_part = jnp.sin(angles)
    former = entries[..., :halfway]
    latter = entries[..., halfway:]
    return jnp.concatenate(
        [former * cosine - latter * sine_part, latter * cosine + former * sine_part], axis=-1
    )


def request_layout(length_row, slot_count):
    end_slot = jnp.cumsum(length_row, dtype=jnp.int32)
    start_slot = end_slot - length_row
    slot_ids = jnp.arange(slot_count, dtype=jnp.int32)
    member = (slot_ids[:, None] >= start_slot[None, :]) & (slot_ids[:, None] < end_slot[None, :])
    segment = jnp.sum((slot_ids[:, None] >= end_slot[None, :]).astype(jnp.int32), axis=1)
    offset = jnp.sum(jnp.where(member, start_slot[None, :], 0), axis=1)
    return (member, segment, slot_ids - offset)


def allowed_pairs(segment):
    slot_ids = jnp.arange(segment.shape[0], dtype=jnp.int32)
    return (segment[:, None] == segment[None, :]) & (slot_ids[None, :] <= slot_ids[:, None])


def attend_heads(query, key_rows, value_rows, positions, allowed, repeat_times):
    slot_count = query.shape[0]
    query = rotate(query.reshape(slot_count, -1, HEAD_DIM).transpose(1, 0, 2), positions).astype(
        jnp.bfloat16
    )
    key_rows = rotate(
        key_rows.reshape(slot_count, -1, HEAD_DIM).transpose(1, 0, 2), positions
    ).astype(jnp.bfloat16)
    value_rows = (
        value_rows.reshape(slot_count, -1, HEAD_DIM).transpose(1, 0, 2).astype(jnp.bfloat16)
    )
    key_rows = jnp.repeat(key_rows, repeat_times, axis=0)
    value_rows = jnp.repeat(value_rows, repeat_times, axis=0)
    scores = jnp.einsum(
        "hqd,hkd->hqk", query.astype(jnp.float32), key_rows.astype(jnp.float32)
    ) * HEAD_DIM ** (-0.5)
    scores = jnp.where(allowed[None], scores, -1e30)
    highest = jnp.max(scores, axis=-1, keepdims=True)
    weights = jnp.exp(scores - highest)
    probs = (weights / jnp.sum(weights, axis=-1, keepdims=True)).astype(jnp.bfloat16)
    attended = jnp.einsum(
        "hqk,hkd->hqd", probs.astype(jnp.float32), value_rows.astype(jnp.float32)
    ).astype(jnp.bfloat16)
    return attended.transpose(1, 0, 2).reshape(slot_count, -1)


def per_device(
    tokens,
    lengths,
    response,
    targets,
    attn_gain,
    w_query,
    w_key,
    w_value,
    output_weight,
    mlp_gain,
    w_gate,
    w_up,
    w_down,
    final_gain,
    w_head,
):
    group_rows = tokens.shape[0]
    own_rows = group_rows // lax.axis_size("mp")
    mp_index = lax.axis_index("mp")
    member, segment, positions = request_layout(lengths[0], group_rows)
    allowed = allowed_pairs(segment)
    heads_here = w_query.shape[2] // HEAD_DIM
    sharing = HEADS // KV_HEADS
    kv_here = max(1, heads_here // sharing)
    kv_first = mp_index * heads_here // sharing * HEAD_DIM
    key_cols = lax.dynamic_slice_in_dim(w_key, kv_first, kv_here * HEAD_DIM, 2)
    value_columns = lax.dynamic_slice_in_dim(w_value, kv_first, kv_here * HEAD_DIM, 2)
    attended_list = []
    for model in range(2):
        normed = rms_scale(tokens, attn_gain[model]).astype(jnp.bfloat16)
        query = jnp.dot(normed, w_query[model], preferred_element_type=jnp.float32)
        keys_here = jnp.dot(normed, key_cols[model], preferred_element_type=jnp.float32)
        values_here = jnp.dot(normed, value_columns[model], preferred_element_type=jnp.float32)
        attended_list.append(
            attend_heads(
                query, keys_here, values_here, positions, allowed, min(sharing, heads_here)
            )
        )
    attended = jnp.stack(attended_list, axis=1)
    selected_rows = attended
    mixed = lax.psum_scatter(
        jnp.einsum(
            "kbq,bqo->kbo", selected_rows, output_weight, preferred_element_type=jnp.float32
        ).astype(jnp.bfloat16),
        "mp",
        scatter_dimension=0,
        tiled=True,
    ).astype(jnp.float32)
    own_tokens = lax.dynamic_slice_in_dim(tokens, mp_index * own_rows, own_rows, 0)
    residual = own_tokens.astype(jnp.float32)[:, None, :] + mixed
    normed_mid = rms_scale(residual, mlp_gain).astype(jnp.bfloat16)
    row_block = lax.all_gather(normed_mid, "mp", axis=0, tiled=True)
    gate_part = jnp.einsum("nmd,mdf->nmf", row_block, w_gate, preferred_element_type=jnp.float32)
    lift_part = jnp.einsum("nmd,mdf->nmf", row_block, w_up, preferred_element_type=jnp.float32)
    hidden = (jax.nn.silu(gate_part) * lift_part).astype(jnp.bfloat16)
    selected_rows = hidden
    final = residual + lax.psum_scatter(
        jnp.einsum(
            "nmf,mfd->nmd", selected_rows, w_down, preferred_element_type=jnp.float32
        ).astype(jnp.bfloat16),
        "mp",
        scatter_dimension=0,
        tiled=True,
    ).astype(jnp.float32)
    closing = rms_scale(final, final_gain).astype(jnp.bfloat16)
    vocab_here = w_head.shape[2]
    vocab_first = lax.axis_index(("req", "mp")) * vocab_here
    column_ids = jnp.arange(vocab_here, dtype=jnp.int32)
    logits = jnp.einsum(
        "nmd,mdv->mnv",
        lax.all_gather(closing, ("req", "mp"), axis=0, tiled=True),
        w_head,
        preferred_element_type=jnp.float32,
    )
    peak_part = jnp.max(logits, axis=-1)
    total_part = jnp.sum(jnp.exp(logits - peak_part[..., None]), axis=-1)
    wanted = targets - vocab_first
    hit_part = jnp.sum(
        jnp.where(column_ids[None, None, :] == wanted[None, :, None], logits, 0.0), axis=-1
    )

    groups = lax.axis_size("req")
    parts = lax.axis_size("mp")
    stats = jnp.stack([peak_part, total_part, hit_part])
    tenant_stats = stats.reshape(3, 2, groups, group_rows).transpose(2, 0, 1, 3)
    outgoing = jnp.broadcast_to(
        tenant_stats[:, None], (groups, parts, 3, 2, group_rows)
    ).reshape(groups * parts, 3, 2, group_rows)
    incoming = lax.all_to_all(outgoing, ("req", "mp"), 0, 0, tiled=True)
    peak_all = jnp.max(incoming[:, 0], axis=0)
    total_all = jnp.sum(incoming[:, 1] * jnp.exp(incoming[:, 0] - peak_all[None]), axis=0)
    hit_all = jnp.sum(incoming[:, 2], axis=0)
    log_likelihood = hit_all - (peak_all + jnp.log(total_all))
    gap = log_likelihood[0] - log_likelihood[1]
    group_gap = gap * response.astype(jnp.float32)
    token_out = lax.dynamic_slice_in_dim(group_gap, mp_index * own_rows, own_rows, 0)
    member_weights = member.astype(jnp.float32)
    request_sum = jnp.dot(group_gap, member_weights, precision=lax.Precision.HIGHEST)
    request_peak = jnp.max(member_weights * jnp.abs(group_gap)[:, None], axis=0)
    return (token_out, request_sum[None, :], request_peak[None, :])


def solution(mesh):
    placed = (
        P("req", None),
        P("req", None),
        P("req"),
        P(),
        P(),
        P(None, None, "mp"),
        P(),
        P(),
        P(None, "mp", None),
        P(),
        P(None, None, "mp"),
        P(None, None, "mp"),
        P(None, "mp", None),
        P(),
        P(None, None, ("req", "mp")),
    )
    return jax.shard_map(
        per_device,
        mesh=mesh,
        in_specs=placed,
        out_specs=(P(("req", "mp")), P("req", None), P("req", None)),
        check_vma=False,
    )
```

```python
import jax
import jax.numpy as jnp
from jax import lax
from jax.sharding import PartitionSpec as P

HEADS = 32
KV_HEADS = 8
HEAD_DIM = 64


epsilon = 1e-05
theta = 500000.0


def merged(part, axis, combine):
    gathered = jax.tree.map(lambda a: lax.all_gather(a, axis), part)

    def take(source):
        return jax.tree.map(lambda a: lax.dynamic_index_in_dim(a, source, 0, False), gathered)

    return lax.fori_loop(
        1, lax.axis_size(axis), lambda source, state: combine(state, take(source)), take(0)
    )


def rms_scale(entries, scaling):
    entries = entries.astype(jnp.float32)
    inverse = lax.rsqrt(jnp.mean(entries * entries, axis=-1, keepdims=True) + epsilon)
    return entries * inverse * scaling


def rotate(entries, positions):
    halfway = entries.shape[-1] // 2
    frequency = theta ** (-jnp.arange(halfway, dtype=jnp.float32) * 2.0 / entries.shape[-1])
    angles = positions.astype(jnp.float32)[:, None] * frequency[None, :]
    cosine = jnp.cos(angles)
    sine_part = jnp.sin(angles)
    former = entries[..., :halfway]
    latter = entries[..., halfway:]
    return jnp.concatenate(
        [former * cosine - latter * sine_part, latter * cosine + former * sine_part], axis=-1
    )


def request_layout(length_row, slot_count):
    end_slot = jnp.cumsum(length_row, dtype=jnp.int32)
    start_slot = end_slot - length_row
    slot_ids = jnp.arange(slot_count, dtype=jnp.int32)
    member = (slot_ids[:, None] >= start_slot[None, :]) & (slot_ids[:, None] < end_slot[None, :])
    segment = jnp.sum((slot_ids[:, None] >= end_slot[None, :]).astype(jnp.int32), axis=1)
    offset = jnp.sum(jnp.where(member, start_slot[None, :], 0), axis=1)
    return (member, segment, slot_ids - offset)


def allowed_pairs(segment):
    slot_ids = jnp.arange(segment.shape[0], dtype=jnp.int32)
    return (segment[:, None] == segment[None, :]) & (slot_ids[None, :] <= slot_ids[:, None])


def attend_heads(query, key_rows, value_rows, positions, allowed, repeat_times):
    slot_count = query.shape[0]
    query = rotate(query.reshape(slot_count, -1, HEAD_DIM).transpose(1, 0, 2), positions).astype(
        jnp.bfloat16
    )
    key_rows = rotate(
        key_rows.reshape(slot_count, -1, HEAD_DIM).transpose(1, 0, 2), positions
    ).astype(jnp.bfloat16)
    value_rows = (
        value_rows.reshape(slot_count, -1, HEAD_DIM).transpose(1, 0, 2).astype(jnp.bfloat16)
    )
    key_rows = jnp.repeat(key_rows, repeat_times, axis=0)
    value_rows = jnp.repeat(value_rows, repeat_times, axis=0)
    scores = jnp.einsum(
        "hqd,hkd->hqk", query.astype(jnp.float32), key_rows.astype(jnp.float32)
    ) * HEAD_DIM ** (-0.5)
    scores = jnp.where(allowed[None], scores, -1e30)
    highest = jnp.max(scores, axis=-1, keepdims=True)
    weights = jnp.exp(scores - highest)
    probs = (weights / jnp.sum(weights, axis=-1, keepdims=True)).astype(jnp.bfloat16)
    attended = jnp.einsum(
        "hqk,hkd->hqd", probs.astype(jnp.float32), value_rows.astype(jnp.float32)
    ).astype(jnp.bfloat16)
    return attended.transpose(1, 0, 2).reshape(slot_count, -1)


def per_device(
    tokens,
    lengths,
    response,
    targets,
    attn_gain,
    w_query,
    w_key,
    w_value,
    output_weight,
    mlp_gain,
    w_gate,
    w_up,
    w_down,
    final_gain,
    w_head,
):
    group_rows = tokens.shape[0]
    own_rows = group_rows // lax.axis_size("mp")
    mp_index = lax.axis_index("mp")
    member, segment, positions = request_layout(lengths[0], group_rows)
    allowed = allowed_pairs(segment)
    heads_here = w_query.shape[2] // HEAD_DIM
    sharing = HEADS // KV_HEADS
    kv_here = max(1, heads_here // sharing)
    kv_first = mp_index * heads_here // sharing * HEAD_DIM
    key_cols = lax.dynamic_slice_in_dim(w_key, kv_first, kv_here * HEAD_DIM, 2)
    value_columns = lax.dynamic_slice_in_dim(w_value, kv_first, kv_here * HEAD_DIM, 2)
    own_tokens = lax.dynamic_slice_in_dim(tokens, mp_index * own_rows, own_rows, 0)
    vocab_here = w_head.shape[2]
    vocab_first = lax.axis_index(("req", "mp")) * vocab_here
    column_ids = jnp.arange(vocab_here, dtype=jnp.int32)
    wanted = targets - vocab_first
    per_model = []
    for model in range(2):
        normed = rms_scale(tokens, attn_gain[model]).astype(jnp.bfloat16)
        query = jnp.dot(normed, w_query[model], preferred_element_type=jnp.float32)
        keys_here = jnp.dot(normed, key_cols[model], preferred_element_type=jnp.float32)
        values_here = jnp.dot(normed, value_columns[model], preferred_element_type=jnp.float32)
        attended = attend_heads(
            query, keys_here, values_here, positions, allowed, min(sharing, heads_here)
        )
        mixed = lax.psum_scatter(
            jnp.dot(
                attended, output_weight[model], preferred_element_type=jnp.float32
            ).astype(jnp.bfloat16),
            "mp",
            scatter_dimension=0,
            tiled=True,
        ).astype(jnp.float32)
        residual = own_tokens.astype(jnp.float32) + mixed
        normed_mid = rms_scale(residual, mlp_gain[model]).astype(jnp.bfloat16)
        row_block = lax.all_gather(normed_mid, "mp", axis=0, tiled=True)
        gate_part = jnp.dot(row_block, w_gate[model], preferred_element_type=jnp.float32)
        lift_part = jnp.dot(row_block, w_up[model], preferred_element_type=jnp.float32)
        hidden = (jax.nn.silu(gate_part) * lift_part).astype(jnp.bfloat16)
        final = residual + lax.psum_scatter(
            jnp.dot(hidden, w_down[model], preferred_element_type=jnp.float32).astype(
                jnp.bfloat16
            ),
            "mp",
            scatter_dimension=0,
            tiled=True,
        ).astype(jnp.float32)
        closing = rms_scale(final, final_gain[model]).astype(jnp.bfloat16)
        logits = jnp.dot(
            lax.all_gather(closing, ("req", "mp"), axis=0, tiled=True),
            w_head[model],
            preferred_element_type=jnp.float32,
        )
        peak_part = jnp.max(logits, axis=-1)
        total_part = jnp.sum(jnp.exp(logits - peak_part[:, None]), axis=-1)
        hit_part = jnp.sum(
            jnp.where(column_ids[None, :] == wanted[:, None], logits, 0.0), axis=-1
        )
        per_model.append(jnp.stack([peak_part, total_part, hit_part]))

    groups = lax.axis_size("req")
    parts = lax.axis_size("mp")
    stats = jnp.stack(per_model, axis=1)
    tenant_stats = stats.reshape(3, 2, groups, group_rows).transpose(2, 0, 1, 3)
    outgoing = jnp.broadcast_to(
        tenant_stats[:, None], (groups, parts, 3, 2, group_rows)
    ).reshape(groups * parts, 3, 2, group_rows)
    incoming = lax.all_to_all(outgoing, ("req", "mp"), 0, 0, tiled=True)
    peak_all = jnp.max(incoming[:, 0], axis=0)
    total_all = jnp.sum(incoming[:, 1] * jnp.exp(incoming[:, 0] - peak_all[None]), axis=0)
    hit_all = jnp.sum(incoming[:, 2], axis=0)
    log_likelihood = hit_all - (peak_all + jnp.log(total_all))
    gap = log_likelihood[0] - log_likelihood[1]
    group_gap = gap * response.astype(jnp.float32)
    token_out = lax.dynamic_slice_in_dim(group_gap, mp_index * own_rows, own_rows, 0)
    member_weights = member.astype(jnp.float32)
    request_sum = jnp.dot(group_gap, member_weights, precision=lax.Precision.HIGHEST)
    request_peak = jnp.max(member_weights * jnp.abs(group_gap)[:, None], axis=0)
    return (token_out, request_sum[None, :], request_peak[None, :])


def solution(mesh):
    placed = (
        P("req", None),
        P("req", None),
        P("req"),
        P(),
        P(),
        P(None, None, "mp"),
        P(),
        P(),
        P(None, "mp", None),
        P(),
        P(None, None, "mp"),
        P(None, None, "mp"),
        P(None, "mp", None),
        P(),
        P(None, None, ("req", "mp")),
    )
    return jax.shard_map(
        per_device,
        mesh=mesh,
        in_specs=placed,
        out_specs=(P(("req", "mp")), P("req", None), P("req", None)),
        check_vma=False,
    )
```

```python
import jax
import jax.numpy as jnp
from jax import lax
from jax.sharding import PartitionSpec as P

HEADS = 32
KV_HEADS = 8
HEAD_DIM = 64


epsilon = 1e-05
theta = 500000.0


def merged(part, axis, combine):
    gathered = jax.tree.map(lambda a: lax.all_gather(a, axis), part)

    def take(source):
        return jax.tree.map(lambda a: lax.dynamic_index_in_dim(a, source, 0, False), gathered)

    return lax.fori_loop(
        1, lax.axis_size(axis), lambda source, state: combine(state, take(source)), take(0)
    )


def rms_scale(entries, scaling):
    entries = entries.astype(jnp.float32)
    inverse = lax.rsqrt(jnp.mean(entries * entries, axis=-1, keepdims=True) + epsilon)
    return entries * inverse * scaling


def rotate(entries, positions):
    halfway = entries.shape[-1] // 2
    frequency = theta ** (-jnp.arange(halfway, dtype=jnp.float32) * 2.0 / entries.shape[-1])
    angles = positions.astype(jnp.float32)[:, None] * frequency[None, :]
    cosine = jnp.cos(angles)
    sine_part = jnp.sin(angles)
    former = entries[..., :halfway]
    latter = entries[..., halfway:]
    return jnp.concatenate(
        [former * cosine - latter * sine_part, latter * cosine + former * sine_part], axis=-1
    )


def request_layout(length_row, slot_count):
    end_slot = jnp.cumsum(length_row, dtype=jnp.int32)
    start_slot = end_slot - length_row
    slot_ids = jnp.arange(slot_count, dtype=jnp.int32)
    member = (slot_ids[:, None] >= start_slot[None, :]) & (slot_ids[:, None] < end_slot[None, :])
    segment = jnp.sum((slot_ids[:, None] >= end_slot[None, :]).astype(jnp.int32), axis=1)
    offset = jnp.sum(jnp.where(member, start_slot[None, :], 0), axis=1)
    return (member, segment, slot_ids - offset)


def allowed_pairs(segment):
    slot_ids = jnp.arange(segment.shape[0], dtype=jnp.int32)
    return (segment[:, None] == segment[None, :]) & (slot_ids[None, :] <= slot_ids[:, None])


def attend_heads(query, key_rows, value_rows, positions, allowed, repeat_times):
    slot_count = query.shape[0]
    query = rotate(query.reshape(slot_count, -1, HEAD_DIM).transpose(1, 0, 2), positions).astype(
        jnp.bfloat16
    )
    key_rows = rotate(
        key_rows.reshape(slot_count, -1, HEAD_DIM).transpose(1, 0, 2), positions
    ).astype(jnp.bfloat16)
    value_rows = (
        value_rows.reshape(slot_count, -1, HEAD_DIM).transpose(1, 0, 2).astype(jnp.bfloat16)
    )
    key_rows = jnp.repeat(key_rows, repeat_times, axis=0)
    value_rows = jnp.repeat(value_rows, repeat_times, axis=0)
    scores = jnp.einsum(
        "hqd,hkd->hqk", query.astype(jnp.float32), key_rows.astype(jnp.float32)
    ) * HEAD_DIM ** (-0.5)
    scores = jnp.where(allowed[None], scores, -1e30)
    highest = jnp.max(scores, axis=-1, keepdims=True)
    weights = jnp.exp(scores - highest)
    probs = (weights / jnp.sum(weights, axis=-1, keepdims=True)).astype(jnp.bfloat16)
    attended = jnp.einsum(
        "hqk,hkd->hqd", probs.astype(jnp.float32), value_rows.astype(jnp.float32)
    ).astype(jnp.bfloat16)
    return attended.transpose(1, 0, 2).reshape(slot_count, -1)


def per_device(
    tokens,
    lengths,
    response,
    targets,
    attn_gain,
    w_query,
    w_key,
    w_value,
    output_weight,
    mlp_gain,
    w_gate,
    w_up,
    w_down,
    final_gain,
    w_head,
):
    group_rows = tokens.shape[0]
    own_rows = group_rows // lax.axis_size("mp")
    mp_index = lax.axis_index("mp")
    member, segment, positions = request_layout(lengths[0], group_rows)
    allowed = allowed_pairs(segment)
    heads_here = w_query.shape[2] // HEAD_DIM
    sharing = HEADS // KV_HEADS
    kv_here = max(1, heads_here // sharing)
    kv_first = mp_index * heads_here // sharing * HEAD_DIM
    key_cols = lax.dynamic_slice_in_dim(w_key, kv_first, kv_here * HEAD_DIM, 2)
    value_columns = lax.dynamic_slice_in_dim(w_value, kv_first, kv_here * HEAD_DIM, 2)
    attended_list = []
    for model in range(2):
        normed = rms_scale(tokens, attn_gain[model]).astype(jnp.bfloat16)
        query = jnp.dot(normed, w_query[model], preferred_element_type=jnp.float32)
        keys_here = jnp.dot(normed, key_cols[model], preferred_element_type=jnp.float32)
        values_here = jnp.dot(normed, value_columns[model], preferred_element_type=jnp.float32)
        attended_list.append(
            attend_heads(
                query, keys_here, values_here, positions, allowed, min(sharing, heads_here)
            )
        )
    attended = jnp.stack(attended_list, axis=1)
    selected_rows = attended
    mixed = lax.psum(
        jnp.einsum(
            "kbq,bqo->kbo", selected_rows, output_weight, preferred_element_type=jnp.float32
        ).astype(jnp.bfloat16),
        "mp",
    ).astype(jnp.float32)
    residual_rows = tokens.astype(jnp.float32)[:, None, :] + mixed
    row_block = rms_scale(residual_rows, mlp_gain).astype(jnp.bfloat16)
    residual = lax.dynamic_slice_in_dim(residual_rows, mp_index * own_rows, own_rows, 0)
    gate_part = jnp.einsum("nmd,mdf->nmf", row_block, w_gate, preferred_element_type=jnp.float32)
    lift_part = jnp.einsum("nmd,mdf->nmf", row_block, w_up, preferred_element_type=jnp.float32)
    hidden = (jax.nn.silu(gate_part) * lift_part).astype(jnp.bfloat16)
    selected_rows = hidden
    final = residual + lax.psum_scatter(
        jnp.einsum(
            "nmf,mfd->nmd", selected_rows, w_down, preferred_element_type=jnp.float32
        ).astype(jnp.bfloat16),
        "mp",
        scatter_dimension=0,
        tiled=True,
    ).astype(jnp.float32)
    closing = rms_scale(final, final_gain).astype(jnp.bfloat16)
    vocab_here = w_head.shape[2]
    vocab_first = lax.axis_index(("req", "mp")) * vocab_here
    column_ids = jnp.arange(vocab_here, dtype=jnp.int32)
    logits = jnp.einsum(
        "nmd,mdv->mnv",
        lax.all_gather(closing, ("req", "mp"), axis=0, tiled=True),
        w_head,
        preferred_element_type=jnp.float32,
    )
    peak_part = jnp.max(logits, axis=-1)
    total_part = jnp.sum(jnp.exp(logits - peak_part[..., None]), axis=-1)
    wanted = targets - vocab_first
    hit_part = jnp.sum(
        jnp.where(column_ids[None, None, :] == wanted[None, :, None], logits, 0.0), axis=-1
    )

    groups = lax.axis_size("req")
    parts = lax.axis_size("mp")
    stats = jnp.stack([peak_part, total_part, hit_part])
    tenant_stats = stats.reshape(3, 2, groups, group_rows).transpose(2, 0, 1, 3)
    outgoing = jnp.broadcast_to(
        tenant_stats[:, None], (groups, parts, 3, 2, group_rows)
    ).reshape(groups * parts, 3, 2, group_rows)
    incoming = lax.all_to_all(outgoing, ("req", "mp"), 0, 0, tiled=True)
    peak_all = jnp.max(incoming[:, 0], axis=0)
    total_all = jnp.sum(incoming[:, 1] * jnp.exp(incoming[:, 0] - peak_all[None]), axis=0)
    hit_all = jnp.sum(incoming[:, 2], axis=0)
    log_likelihood = hit_all - (peak_all + jnp.log(total_all))
    gap = log_likelihood[0] - log_likelihood[1]
    group_gap = gap * response.astype(jnp.float32)
    token_out = lax.dynamic_slice_in_dim(group_gap, mp_index * own_rows, own_rows, 0)
    member_weights = member.astype(jnp.float32)
    request_sum = jnp.dot(group_gap, member_weights, precision=lax.Precision.HIGHEST)
    request_peak = jnp.max(member_weights * jnp.abs(group_gap)[:, None], axis=0)
    return (token_out, request_sum[None, :], request_peak[None, :])


def solution(mesh):
    placed = (
        P("req", None),
        P("req", None),
        P("req"),
        P(),
        P(),
        P(None, None, "mp"),
        P(),
        P(),
        P(None, "mp", None),
        P(),
        P(None, None, "mp"),
        P(None, None, "mp"),
        P(None, "mp", None),
        P(),
        P(None, None, ("req", "mp")),
    )
    return jax.shard_map(
        per_device,
        mesh=mesh,
        in_specs=placed,
        out_specs=(P(("req", "mp")), P("req", None), P("req", None)),
        check_vma=False,
    )
```

```python
import jax
import jax.numpy as jnp
from jax import lax
from jax.sharding import PartitionSpec as P

HEADS = 32
KV_HEADS = 8
HEAD_DIM = 64


epsilon = 1e-05
theta = 500000.0


def merged(part, axis, combine):
    gathered = jax.tree.map(lambda a: lax.all_gather(a, axis), part)

    def take(source):
        return jax.tree.map(lambda a: lax.dynamic_index_in_dim(a, source, 0, False), gathered)

    return lax.fori_loop(
        1, lax.axis_size(axis), lambda source, state: combine(state, take(source)), take(0)
    )


def rms_scale(entries, scaling):
    entries = entries.astype(jnp.float32)
    inverse = lax.rsqrt(jnp.mean(entries * entries, axis=-1, keepdims=True) + epsilon)
    return entries * inverse * scaling


def rotate(entries, positions):
    halfway = entries.shape[-1] // 2
    frequency = theta ** (-jnp.arange(halfway, dtype=jnp.float32) * 2.0 / entries.shape[-1])
    angles = positions.astype(jnp.float32)[:, None] * frequency[None, :]
    cosine = jnp.cos(angles)
    sine_part = jnp.sin(angles)
    former = entries[..., :halfway]
    latter = entries[..., halfway:]
    return jnp.concatenate(
        [former * cosine - latter * sine_part, latter * cosine + former * sine_part], axis=-1
    )


def request_layout(length_row, slot_count):
    end_slot = jnp.cumsum(length_row, dtype=jnp.int32)
    start_slot = end_slot - length_row
    slot_ids = jnp.arange(slot_count, dtype=jnp.int32)
    member = (slot_ids[:, None] >= start_slot[None, :]) & (slot_ids[:, None] < end_slot[None, :])
    segment = jnp.sum((slot_ids[:, None] >= end_slot[None, :]).astype(jnp.int32), axis=1)
    offset = jnp.sum(jnp.where(member, start_slot[None, :], 0), axis=1)
    return (member, segment, slot_ids - offset)


def allowed_pairs(segment):
    slot_ids = jnp.arange(segment.shape[0], dtype=jnp.int32)
    return (segment[:, None] == segment[None, :]) & (slot_ids[None, :] <= slot_ids[:, None])


def attend_heads(query, key_rows, value_rows, positions, allowed, repeat_times):
    slot_count = query.shape[0]
    query = rotate(query.reshape(slot_count, -1, HEAD_DIM).transpose(1, 0, 2), positions).astype(
        jnp.bfloat16
    )
    key_rows = rotate(
        key_rows.reshape(slot_count, -1, HEAD_DIM).transpose(1, 0, 2), positions
    ).astype(jnp.bfloat16)
    value_rows = (
        value_rows.reshape(slot_count, -1, HEAD_DIM).transpose(1, 0, 2).astype(jnp.bfloat16)
    )
    key_rows = jnp.repeat(key_rows, repeat_times, axis=0)
    value_rows = jnp.repeat(value_rows, repeat_times, axis=0)
    scores = jnp.einsum(
        "hqd,hkd->hqk", query, key_rows, preferred_element_type=jnp.float32
    ) * HEAD_DIM ** (-0.5)
    scores = jnp.where(allowed[None], scores, -1e30)
    highest = jnp.max(scores, axis=-1, keepdims=True)
    weights = jnp.exp(scores - highest)
    probs = (weights / jnp.sum(weights, axis=-1, keepdims=True)).astype(jnp.bfloat16)
    attended = jnp.einsum(
        "hqk,hkd->hqd", probs, value_rows, preferred_element_type=jnp.float32
    ).astype(jnp.bfloat16)
    return attended.transpose(1, 0, 2).reshape(slot_count, -1)


def per_device(
    tokens,
    lengths,
    response,
    targets,
    attn_gain,
    w_query,
    w_key,
    w_value,
    output_weight,
    mlp_gain,
    w_gate,
    w_up,
    w_down,
    final_gain,
    w_head,
):
    group_rows = tokens.shape[0]
    own_rows = group_rows // lax.axis_size("mp")
    mp_index = lax.axis_index("mp")
    member, segment, positions = request_layout(lengths[0], group_rows)
    allowed = allowed_pairs(segment)
    heads_here = w_query.shape[2] // HEAD_DIM
    sharing = HEADS // KV_HEADS
    kv_here = max(1, heads_here // sharing)
    kv_first = mp_index * heads_here // sharing * HEAD_DIM
    key_cols = lax.dynamic_slice_in_dim(w_key, kv_first, kv_here * HEAD_DIM, 2)
    value_columns = lax.dynamic_slice_in_dim(w_value, kv_first, kv_here * HEAD_DIM, 2)
    attended_list = []
    for model in range(2):
        normed = rms_scale(tokens, attn_gain[model]).astype(jnp.bfloat16)
        query = jnp.dot(normed, w_query[model], preferred_element_type=jnp.float32)
        keys_here = jnp.dot(normed, key_cols[model], preferred_element_type=jnp.float32)
        values_here = jnp.dot(normed, value_columns[model], preferred_element_type=jnp.float32)
        attended_list.append(
            attend_heads(
                query, keys_here, values_here, positions, allowed, min(sharing, heads_here)
            )
        )
    attended = jnp.stack(attended_list, axis=1)
    selected_rows = attended
    mixed = lax.psum_scatter(
        jnp.einsum(
            "kbq,bqo->kbo", selected_rows, output_weight, preferred_element_type=jnp.float32
        ).astype(jnp.bfloat16),
        "mp",
        scatter_dimension=0,
        tiled=True,
    ).astype(jnp.float32)
    own_tokens = lax.dynamic_slice_in_dim(tokens, mp_index * own_rows, own_rows, 0)
    residual = own_tokens.astype(jnp.float32)[:, None, :] + mixed
    normed_mid = rms_scale(residual, mlp_gain).astype(jnp.bfloat16)
    row_block = lax.all_gather(normed_mid, "mp", axis=0, tiled=True)
    gate_part = jnp.einsum("nmd,mdf->nmf", row_block, w_gate, preferred_element_type=jnp.float32)
    lift_part = jnp.einsum("nmd,mdf->nmf", row_block, w_up, preferred_element_type=jnp.float32)
    hidden = (jax.nn.silu(gate_part) * lift_part).astype(jnp.bfloat16)
    selected_rows = hidden
    final = residual + lax.psum_scatter(
        jnp.einsum(
            "nmf,mfd->nmd", selected_rows, w_down, preferred_element_type=jnp.float32
        ).astype(jnp.bfloat16),
        "mp",
        scatter_dimension=0,
        tiled=True,
    ).astype(jnp.float32)
    closing = rms_scale(final, final_gain).astype(jnp.bfloat16)
    vocab_here = w_head.shape[2]
    vocab_first = lax.axis_index(("req", "mp")) * vocab_here
    column_ids = jnp.arange(vocab_here, dtype=jnp.int32)
    logits = jnp.einsum(
        "nmd,mdv->mnv",
        lax.all_gather(closing, ("req", "mp"), axis=0, tiled=True),
        w_head,
        preferred_element_type=jnp.float32,
    )
    peak_part = jnp.max(logits, axis=-1)
    total_part = jnp.sum(jnp.exp(logits - peak_part[..., None]), axis=-1)
    wanted = targets - vocab_first
    hit_part = jnp.sum(
        jnp.where(column_ids[None, None, :] == wanted[None, :, None], logits, 0.0), axis=-1
    )

    groups = lax.axis_size("req")
    parts = lax.axis_size("mp")
    stats = jnp.stack([peak_part, total_part, hit_part])
    tenant_stats = stats.reshape(3, 2, groups, group_rows).transpose(2, 0, 1, 3)
    outgoing = jnp.broadcast_to(
        tenant_stats[:, None], (groups, parts, 3, 2, group_rows)
    ).reshape(groups * parts, 3, 2, group_rows)
    incoming = lax.all_to_all(outgoing, ("req", "mp"), 0, 0, tiled=True)
    peak_all = jnp.max(incoming[:, 0], axis=0)
    total_all = jnp.sum(incoming[:, 1] * jnp.exp(incoming[:, 0] - peak_all[None]), axis=0)
    hit_all = jnp.sum(incoming[:, 2], axis=0)
    log_likelihood = hit_all - (peak_all + jnp.log(total_all))
    gap = log_likelihood[0] - log_likelihood[1]
    group_gap = gap * response.astype(jnp.float32)
    token_out = lax.dynamic_slice_in_dim(group_gap, mp_index * own_rows, own_rows, 0)
    member_weights = member.astype(jnp.float32)
    request_sum = jnp.dot(group_gap, member_weights, precision=lax.Precision.HIGHEST)
    request_peak = jnp.max(member_weights * jnp.abs(group_gap)[:, None], axis=0)
    return (token_out, request_sum[None, :], request_peak[None, :])


def solution(mesh):
    placed = (
        P("req", None),
        P("req", None),
        P("req"),
        P(),
        P(),
        P(None, None, "mp"),
        P(),
        P(),
        P(None, "mp", None),
        P(),
        P(None, None, "mp"),
        P(None, None, "mp"),
        P(None, "mp", None),
        P(),
        P(None, None, ("req", "mp")),
    )
    return jax.shard_map(
        per_device,
        mesh=mesh,
        in_specs=placed,
        out_specs=(P(("req", "mp")), P("req", None), P("req", None)),
        check_vma=False,
    )
```

```python
import jax
import jax.numpy as jnp
from jax import lax
from jax.sharding import PartitionSpec as P

HEADS = 32
KV_HEADS = 8
HEAD_DIM = 64


epsilon = 1e-05
theta = 500000.0


def merged(part, axis, combine):
    gathered = jax.tree.map(lambda a: lax.all_gather(a, axis), part)

    def take(source):
        return jax.tree.map(lambda a: lax.dynamic_index_in_dim(a, source, 0, False), gathered)

    return lax.fori_loop(
        1, lax.axis_size(axis), lambda source, state: combine(state, take(source)), take(0)
    )


def rms_scale(entries, scaling):
    entries = entries.astype(jnp.float32)
    inverse = lax.rsqrt(jnp.mean(entries * entries, axis=-1, keepdims=True) + epsilon)
    return entries * inverse * scaling


def rotate(entries, positions):
    halfway = entries.shape[-1] // 2
    frequency = theta ** (-jnp.arange(halfway, dtype=jnp.float32) * 2.0 / entries.shape[-1])
    angles = positions.astype(jnp.float32)[:, None] * frequency[None, :]
    cosine = jnp.cos(angles)
    sine_part = jnp.sin(angles)
    former = entries[..., :halfway]
    latter = entries[..., halfway:]
    return jnp.concatenate(
        [former * cosine - latter * sine_part, latter * cosine + former * sine_part], axis=-1
    )


def request_layout(length_row, slot_count):
    end_slot = jnp.cumsum(length_row, dtype=jnp.int32)
    start_slot = end_slot - length_row
    slot_ids = jnp.arange(slot_count, dtype=jnp.int32)
    member = (slot_ids[:, None] >= start_slot[None, :]) & (slot_ids[:, None] < end_slot[None, :])
    segment = jnp.sum((slot_ids[:, None] >= end_slot[None, :]).astype(jnp.int32), axis=1)
    offset = jnp.sum(jnp.where(member, start_slot[None, :], 0), axis=1)
    return (member, segment, slot_ids - offset)


def allowed_pairs(segment):
    slot_ids = jnp.arange(segment.shape[0], dtype=jnp.int32)
    return (segment[:, None] == segment[None, :]) & (slot_ids[None, :] <= slot_ids[:, None])


def attend_heads(query, key_rows, value_rows, positions, allowed, repeat_times):
    slot_count = query.shape[1]
    query = rotate(query, positions).astype(jnp.bfloat16)
    key_rows = rotate(key_rows, positions).astype(jnp.bfloat16)
    value_rows = value_rows.astype(jnp.bfloat16)
    key_rows = jnp.repeat(key_rows, repeat_times, axis=0)
    value_rows = jnp.repeat(value_rows, repeat_times, axis=0)
    scores = jnp.einsum(
        "hqd,hkd->hqk", query, key_rows, preferred_element_type=jnp.float32
    ) * HEAD_DIM ** (-0.5)
    scores = jnp.where(allowed[None], scores, -1e30)
    highest = jnp.max(scores, axis=-1, keepdims=True)
    weights = jnp.exp(scores - highest)
    probs = (weights / jnp.sum(weights, axis=-1, keepdims=True)).astype(jnp.bfloat16)
    attended = jnp.einsum(
        "hqk,hkd->hqd", probs, value_rows, preferred_element_type=jnp.float32
    ).astype(jnp.bfloat16)
    return attended.transpose(1, 0, 2).reshape(slot_count, -1)


def per_device(
    tokens,
    lengths,
    response,
    targets,
    attn_gain,
    w_query,
    w_key,
    w_value,
    output_weight,
    mlp_gain,
    w_gate,
    w_up,
    w_down,
    final_gain,
    w_head,
):
    group_rows = tokens.shape[0]
    own_rows = group_rows // lax.axis_size("mp")
    mp_index = lax.axis_index("mp")
    member, segment, positions = request_layout(lengths[0], group_rows)
    allowed = allowed_pairs(segment)
    heads_here = w_query.shape[2] // HEAD_DIM
    sharing = HEADS // KV_HEADS
    kv_here = max(1, heads_here // sharing)
    kv_first = mp_index * heads_here // sharing * HEAD_DIM
    key_cols = lax.dynamic_slice_in_dim(w_key, kv_first, kv_here * HEAD_DIM, 2)
    value_columns = lax.dynamic_slice_in_dim(w_value, kv_first, kv_here * HEAD_DIM, 2)
    attended_list = []
    for model in range(2):
        normed = rms_scale(tokens, attn_gain[model]).astype(jnp.bfloat16)
        width = normed.shape[1]
        query = jnp.einsum(
            "td,dhe->hte",
            normed,
            w_query[model].reshape(width, heads_here, HEAD_DIM),
            preferred_element_type=jnp.float32,
        )
        keys_here = jnp.einsum(
            "td,dhe->hte",
            normed,
            key_cols[model].reshape(width, kv_here, HEAD_DIM),
            preferred_element_type=jnp.float32,
        )
        values_here = jnp.einsum(
            "td,dhe->hte",
            normed,
            value_columns[model].reshape(width, kv_here, HEAD_DIM),
            preferred_element_type=jnp.float32,
        )
        attended_list.append(
            attend_heads(
                query, keys_here, values_here, positions, allowed, min(sharing, heads_here)
            )
        )
    attended = jnp.stack(attended_list, axis=1)
    selected_rows = attended
    mixed = lax.psum_scatter(
        jnp.einsum(
            "kbq,bqo->kbo", selected_rows, output_weight, preferred_element_type=jnp.float32
        ).astype(jnp.bfloat16),
        "mp",
        scatter_dimension=0,
        tiled=True,
    ).astype(jnp.float32)
    own_tokens = lax.dynamic_slice_in_dim(tokens, mp_index * own_rows, own_rows, 0)
    residual = own_tokens.astype(jnp.float32)[:, None, :] + mixed
    normed_mid = rms_scale(residual, mlp_gain).astype(jnp.bfloat16)
    row_block = lax.all_gather(normed_mid, "mp", axis=0, tiled=True)
    gate_part = jnp.einsum("nmd,mdf->nmf", row_block, w_gate, preferred_element_type=jnp.float32)
    lift_part = jnp.einsum("nmd,mdf->nmf", row_block, w_up, preferred_element_type=jnp.float32)
    hidden = (jax.nn.silu(gate_part) * lift_part).astype(jnp.bfloat16)
    selected_rows = hidden
    final = residual + lax.psum_scatter(
        jnp.einsum(
            "nmf,mfd->nmd", selected_rows, w_down, preferred_element_type=jnp.float32
        ).astype(jnp.bfloat16),
        "mp",
        scatter_dimension=0,
        tiled=True,
    ).astype(jnp.float32)
    closing = rms_scale(final, final_gain).astype(jnp.bfloat16)
    vocab_here = w_head.shape[2]
    vocab_first = lax.axis_index(("req", "mp")) * vocab_here
    column_ids = jnp.arange(vocab_here, dtype=jnp.int32)
    logits = jnp.einsum(
        "nmd,mdv->mnv",
        lax.all_gather(closing, ("req", "mp"), axis=0, tiled=True),
        w_head,
        preferred_element_type=jnp.float32,
    )
    peak_part = jnp.max(logits, axis=-1)
    total_part = jnp.sum(jnp.exp(logits - peak_part[..., None]), axis=-1)
    wanted = targets - vocab_first
    hit_part = jnp.sum(
        jnp.where(column_ids[None, None, :] == wanted[None, :, None], logits, 0.0), axis=-1
    )

    groups = lax.axis_size("req")
    parts = lax.axis_size("mp")
    stats = jnp.stack([peak_part, total_part, hit_part])
    tenant_stats = stats.reshape(3, 2, groups, group_rows).transpose(2, 0, 1, 3)
    outgoing = jnp.broadcast_to(
        tenant_stats[:, None], (groups, parts, 3, 2, group_rows)
    ).reshape(groups * parts, 3, 2, group_rows)
    incoming = lax.all_to_all(outgoing, ("req", "mp"), 0, 0, tiled=True)
    peak_all = jnp.max(incoming[:, 0], axis=0)
    total_all = jnp.sum(incoming[:, 1] * jnp.exp(incoming[:, 0] - peak_all[None]), axis=0)
    hit_all = jnp.sum(incoming[:, 2], axis=0)
    log_likelihood = hit_all - (peak_all + jnp.log(total_all))
    gap = log_likelihood[0] - log_likelihood[1]
    group_gap = gap * response.astype(jnp.float32)
    token_out = lax.dynamic_slice_in_dim(group_gap, mp_index * own_rows, own_rows, 0)
    member_weights = member.astype(jnp.float32)
    request_sum = jnp.dot(group_gap, member_weights, precision=lax.Precision.HIGHEST)
    request_peak = jnp.max(member_weights * jnp.abs(group_gap)[:, None], axis=0)
    return (token_out, request_sum[None, :], request_peak[None, :])


def solution(mesh):
    placed = (
        P("req", None),
        P("req", None),
        P("req"),
        P(),
        P(),
        P(None, None, "mp"),
        P(),
        P(),
        P(None, "mp", None),
        P(),
        P(None, None, "mp"),
        P(None, None, "mp"),
        P(None, "mp", None),
        P(),
        P(None, None, ("req", "mp")),
    )
    return jax.shard_map(
        per_device,
        mesh=mesh,
        in_specs=placed,
        out_specs=(P(("req", "mp")), P("req", None), P("req", None)),
        check_vma=False,
    )
```

```python
import jax
import jax.numpy as jnp
from jax import lax
from jax.sharding import PartitionSpec as P

HEADS = 32
KV_HEADS = 8
HEAD_DIM = 64


epsilon = 1e-05
theta = 500000.0


def merged(part, axis, combine):
    gathered = jax.tree.map(lambda a: lax.all_gather(a, axis), part)

    def take(source):
        return jax.tree.map(lambda a: lax.dynamic_index_in_dim(a, source, 0, False), gathered)

    return lax.fori_loop(
        1, lax.axis_size(axis), lambda source, state: combine(state, take(source)), take(0)
    )


def rms_scale(entries, scaling):
    entries = entries.astype(jnp.float32)
    inverse = lax.rsqrt(jnp.mean(entries * entries, axis=-1, keepdims=True) + epsilon)
    return entries * inverse * scaling


def rotate(entries, positions):
    halfway = entries.shape[-1] // 2
    frequency = theta ** (-jnp.arange(halfway, dtype=jnp.float32) * 2.0 / entries.shape[-1])
    angles = positions.astype(jnp.float32)[:, None] * frequency[None, :]
    cosine = jnp.cos(angles)
    sine_part = jnp.sin(angles)
    former = entries[..., :halfway]
    latter = entries[..., halfway:]
    return jnp.concatenate(
        [former * cosine - latter * sine_part, latter * cosine + former * sine_part], axis=-1
    )


def request_layout(length_row, slot_count):
    end_slot = jnp.cumsum(length_row, dtype=jnp.int32)
    start_slot = end_slot - length_row
    slot_ids = jnp.arange(slot_count, dtype=jnp.int32)
    member = (slot_ids[:, None] >= start_slot[None, :]) & (slot_ids[:, None] < end_slot[None, :])
    segment = jnp.sum((slot_ids[:, None] >= end_slot[None, :]).astype(jnp.int32), axis=1)
    offset = jnp.sum(jnp.where(member, start_slot[None, :], 0), axis=1)
    return (member, segment, slot_ids - offset)


def allowed_pairs(segment):
    slot_ids = jnp.arange(segment.shape[0], dtype=jnp.int32)
    return (segment[:, None] == segment[None, :]) & (slot_ids[None, :] <= slot_ids[:, None])


def attend_heads(query, key_rows, value_rows, positions, allowed, repeat_times):
    slot_count = query.shape[1]
    query = rotate(query, positions).astype(jnp.bfloat16)
    key_rows = rotate(key_rows, positions).astype(jnp.bfloat16)
    value_rows = value_rows.astype(jnp.bfloat16)
    key_rows = jnp.repeat(key_rows, repeat_times, axis=0)
    value_rows = jnp.repeat(value_rows, repeat_times, axis=0)
    scores = jnp.einsum(
        "hqd,hkd->hqk", query, key_rows, preferred_element_type=jnp.float32
    ) * HEAD_DIM ** (-0.5)
    scores = jnp.where(allowed[None], scores, -1e30)
    highest = jnp.max(scores, axis=-1, keepdims=True)
    weights = jnp.exp(scores - highest)
    probs = (weights / jnp.sum(weights, axis=-1, keepdims=True)).astype(jnp.bfloat16)
    attended = jnp.einsum(
        "hqk,hkd->hqd", probs, value_rows, preferred_element_type=jnp.float32
    ).astype(jnp.bfloat16)
    return attended.transpose(1, 0, 2).reshape(slot_count, -1)


def per_device(
    tokens,
    lengths,
    response,
    targets,
    attn_gain,
    w_query,
    w_key,
    w_value,
    output_weight,
    mlp_gain,
    w_gate,
    w_up,
    w_down,
    final_gain,
    w_head,
):
    group_rows = tokens.shape[0]
    own_rows = group_rows // lax.axis_size("mp")
    mp_index = lax.axis_index("mp")
    member, segment, positions = request_layout(lengths[0], group_rows)
    allowed = allowed_pairs(segment)
    heads_here = w_query.shape[2] // HEAD_DIM
    sharing = HEADS // KV_HEADS
    kv_here = max(1, heads_here // sharing)
    kv_first = mp_index * heads_here // sharing * HEAD_DIM
    key_cols = lax.dynamic_slice_in_dim(w_key, kv_first, kv_here * HEAD_DIM, 2)
    value_columns = lax.dynamic_slice_in_dim(w_value, kv_first, kv_here * HEAD_DIM, 2)
    attended_list = []
    normed = rms_scale(tokens[None], attn_gain[:, None, :]).astype(jnp.bfloat16)
    width = tokens.shape[1]
    query = jnp.einsum(
        "mtd,mdhe->mhte",
        normed,
        w_query.reshape(2, width, heads_here, HEAD_DIM),
        preferred_element_type=jnp.float32,
    )
    keys_here = jnp.einsum(
        "mtd,mdhe->mhte",
        normed,
        key_cols.reshape(2, width, kv_here, HEAD_DIM),
        preferred_element_type=jnp.float32,
    )
    values_here = jnp.einsum(
        "mtd,mdhe->mhte",
        normed,
        value_columns.reshape(2, width, kv_here, HEAD_DIM),
        preferred_element_type=jnp.float32,
    )
    for model in range(2):
        attended_list.append(
            attend_heads(
                query[model],
                keys_here[model],
                values_here[model],
                positions,
                allowed,
                min(sharing, heads_here),
            )
        )
    attended = jnp.stack(attended_list, axis=1)
    selected_rows = attended
    mixed = lax.psum_scatter(
        jnp.einsum(
            "kbq,bqo->kbo", selected_rows, output_weight, preferred_element_type=jnp.float32
        ).astype(jnp.bfloat16),
        "mp",
        scatter_dimension=0,
        tiled=True,
    ).astype(jnp.float32)
    own_tokens = lax.dynamic_slice_in_dim(tokens, mp_index * own_rows, own_rows, 0)
    residual = own_tokens.astype(jnp.float32)[:, None, :] + mixed
    normed_mid = rms_scale(residual, mlp_gain).astype(jnp.bfloat16)
    row_block = lax.all_gather(normed_mid, "mp", axis=0, tiled=True)
    gate_part = jnp.einsum("nmd,mdf->nmf", row_block, w_gate, preferred_element_type=jnp.float32)
    lift_part = jnp.einsum("nmd,mdf->nmf", row_block, w_up, preferred_element_type=jnp.float32)
    hidden = (jax.nn.silu(gate_part) * lift_part).astype(jnp.bfloat16)
    selected_rows = hidden
    final = residual + lax.psum_scatter(
        jnp.einsum(
            "nmf,mfd->nmd", selected_rows, w_down, preferred_element_type=jnp.float32
        ).astype(jnp.bfloat16),
        "mp",
        scatter_dimension=0,
        tiled=True,
    ).astype(jnp.float32)
    closing = rms_scale(final, final_gain).astype(jnp.bfloat16)
    vocab_here = w_head.shape[2]
    vocab_first = lax.axis_index(("req", "mp")) * vocab_here
    column_ids = jnp.arange(vocab_here, dtype=jnp.int32)
    logits = jnp.einsum(
        "nmd,mdv->mnv",
        lax.all_gather(closing, ("req", "mp"), axis=0, tiled=True),
        w_head,
        preferred_element_type=jnp.float32,
    )
    peak_part = jnp.max(logits, axis=-1)
    total_part = jnp.sum(jnp.exp(logits - peak_part[..., None]), axis=-1)
    wanted = targets - vocab_first
    hit_part = jnp.sum(
        jnp.where(column_ids[None, None, :] == wanted[None, :, None], logits, 0.0), axis=-1
    )

    groups = lax.axis_size("req")
    parts = lax.axis_size("mp")
    stats = jnp.stack([peak_part, total_part, hit_part])
    tenant_stats = stats.reshape(3, 2, groups, group_rows).transpose(2, 0, 1, 3)
    outgoing = jnp.broadcast_to(
        tenant_stats[:, None], (groups, parts, 3, 2, group_rows)
    ).reshape(groups * parts, 3, 2, group_rows)
    incoming = lax.all_to_all(outgoing, ("req", "mp"), 0, 0, tiled=True)
    peak_all = jnp.max(incoming[:, 0], axis=0)
    total_all = jnp.sum(incoming[:, 1] * jnp.exp(incoming[:, 0] - peak_all[None]), axis=0)
    hit_all = jnp.sum(incoming[:, 2], axis=0)
    log_likelihood = hit_all - (peak_all + jnp.log(total_all))
    gap = log_likelihood[0] - log_likelihood[1]
    group_gap = gap * response.astype(jnp.float32)
    token_out = lax.dynamic_slice_in_dim(group_gap, mp_index * own_rows, own_rows, 0)
    member_weights = member.astype(jnp.float32)
    request_sum = jnp.dot(group_gap, member_weights, precision=lax.Precision.HIGHEST)
    request_peak = jnp.max(member_weights * jnp.abs(group_gap)[:, None], axis=0)
    return (token_out, request_sum[None, :], request_peak[None, :])


def solution(mesh):
    placed = (
        P("req", None),
        P("req", None),
        P("req"),
        P(),
        P(),
        P(None, None, "mp"),
        P(),
        P(),
        P(None, "mp", None),
        P(),
        P(None, None, "mp"),
        P(None, None, "mp"),
        P(None, "mp", None),
        P(),
        P(None, None, ("req", "mp")),
    )
    return jax.shard_map(
        per_device,
        mesh=mesh,
        in_specs=placed,
        out_specs=(P(("req", "mp")), P("req", None), P("req", None)),
        check_vma=False,
    )
```

```python
import jax
import jax.numpy as jnp
from jax import lax
from jax.sharding import PartitionSpec as P

HEADS = 32
KV_HEADS = 8
HEAD_DIM = 64


epsilon = 1e-05
theta = 500000.0


def merged(part, axis, combine):
    gathered = jax.tree.map(lambda a: lax.all_gather(a, axis), part)

    def take(source):
        return jax.tree.map(lambda a: lax.dynamic_index_in_dim(a, source, 0, False), gathered)

    return lax.fori_loop(
        1, lax.axis_size(axis), lambda source, state: combine(state, take(source)), take(0)
    )


def rms_scale(entries, scaling):
    entries = entries.astype(jnp.float32)
    inverse = lax.rsqrt(jnp.mean(entries * entries, axis=-1, keepdims=True) + epsilon)
    return entries * inverse * scaling


def rotate(entries, positions):
    halfway = entries.shape[-1] // 2
    frequency = theta ** (-jnp.arange(halfway, dtype=jnp.float32) * 2.0 / entries.shape[-1])
    angles = positions.astype(jnp.float32)[:, None] * frequency[None, :]
    cosine = jnp.cos(angles)
    sine_part = jnp.sin(angles)
    former = entries[..., :halfway]
    latter = entries[..., halfway:]
    return jnp.concatenate(
        [former * cosine - latter * sine_part, latter * cosine + former * sine_part], axis=-1
    )


def request_layout(length_row, slot_count):
    end_slot = jnp.cumsum(length_row, dtype=jnp.int32)
    start_slot = end_slot - length_row
    slot_ids = jnp.arange(slot_count, dtype=jnp.int32)
    member = (slot_ids[:, None] >= start_slot[None, :]) & (slot_ids[:, None] < end_slot[None, :])
    segment = jnp.sum((slot_ids[:, None] >= end_slot[None, :]).astype(jnp.int32), axis=1)
    offset = jnp.sum(jnp.where(member, start_slot[None, :], 0), axis=1)
    return (member, segment, slot_ids - offset)


def allowed_pairs(segment):
    slot_ids = jnp.arange(segment.shape[0], dtype=jnp.int32)
    return (segment[:, None] == segment[None, :]) & (slot_ids[None, :] <= slot_ids[:, None])


def attend_heads(query, key_rows, value_rows, positions, allowed, repeat_times):
    slot_count = query.shape[1]
    query = rotate(query, positions).astype(jnp.bfloat16)
    key_rows = rotate(key_rows, positions).astype(jnp.bfloat16)
    value_rows = value_rows.astype(jnp.bfloat16)
    key_rows = jnp.repeat(key_rows, repeat_times, axis=0)
    value_rows = jnp.repeat(value_rows, repeat_times, axis=0)
    scores = jnp.einsum(
        "hqd,hkd->hqk", query, key_rows, preferred_element_type=jnp.float32
    ) * HEAD_DIM ** (-0.5)
    scores = jnp.where(allowed[None], scores, -1e30)
    highest = jnp.max(scores, axis=-1, keepdims=True)
    weights = jnp.exp(scores - highest)
    probs = (weights / jnp.sum(weights, axis=-1, keepdims=True)).astype(jnp.bfloat16)
    attended = jnp.einsum(
        "hqk,hkd->hqd", probs, value_rows, preferred_element_type=jnp.float32
    ).astype(jnp.bfloat16)
    return attended.transpose(1, 0, 2).reshape(slot_count, -1)


def per_device(
    tokens,
    lengths,
    response,
    targets,
    attn_gain,
    w_query,
    w_key,
    w_value,
    output_weight,
    mlp_gain,
    w_gate,
    w_up,
    w_down,
    final_gain,
    w_head,
):
    group_rows = tokens.shape[0]
    own_rows = group_rows // lax.axis_size("mp")
    mp_index = lax.axis_index("mp")
    member, segment, positions = request_layout(lengths[0], group_rows)
    allowed = allowed_pairs(segment)
    heads_here = w_query.shape[2] // HEAD_DIM
    sharing = HEADS // KV_HEADS
    kv_here = max(1, heads_here // sharing)
    kv_first = mp_index * heads_here // sharing * HEAD_DIM
    attended_list = []
    normed = rms_scale(tokens[None], attn_gain[:, None, :]).astype(jnp.bfloat16)
    width = tokens.shape[1]
    query = jnp.einsum(
        "mtd,mdhe->mhte",
        normed,
        w_query.reshape(2, width, heads_here, HEAD_DIM),
        preferred_element_type=jnp.float32,
    )
    kv_heads = w_key.shape[2] // HEAD_DIM
    kv_head_first = kv_first // HEAD_DIM
    keys_here = lax.dynamic_slice_in_dim(
        jnp.einsum(
            "mtd,mdhe->mhte",
            normed,
            w_key.reshape(2, width, kv_heads, HEAD_DIM),
            preferred_element_type=jnp.float32,
        ),
        kv_head_first,
        kv_here,
        1,
    )
    values_here = lax.dynamic_slice_in_dim(
        jnp.einsum(
            "mtd,mdhe->mhte",
            normed,
            w_value.reshape(2, width, kv_heads, HEAD_DIM),
            preferred_element_type=jnp.float32,
        ),
        kv_head_first,
        kv_here,
        1,
    )
    for model in range(2):
        attended_list.append(
            attend_heads(
                query[model],
                keys_here[model],
                values_here[model],
                positions,
                allowed,
                min(sharing, heads_here),
            )
        )
    attended = jnp.stack(attended_list, axis=1)
    selected_rows = attended
    mixed = lax.psum_scatter(
        jnp.einsum(
            "kbq,bqo->kbo", selected_rows, output_weight, preferred_element_type=jnp.float32
        ).astype(jnp.bfloat16),
        "mp",
        scatter_dimension=0,
        tiled=True,
    ).astype(jnp.float32)
    own_tokens = lax.dynamic_slice_in_dim(tokens, mp_index * own_rows, own_rows, 0)
    residual = own_tokens.astype(jnp.float32)[:, None, :] + mixed
    normed_mid = rms_scale(residual, mlp_gain).astype(jnp.bfloat16)
    row_block = lax.all_gather(normed_mid, "mp", axis=0, tiled=True)
    gate_part = jnp.einsum("nmd,mdf->nmf", row_block, w_gate, preferred_element_type=jnp.float32)
    lift_part = jnp.einsum("nmd,mdf->nmf", row_block, w_up, preferred_element_type=jnp.float32)
    hidden = (jax.nn.silu(gate_part) * lift_part).astype(jnp.bfloat16)
    selected_rows = hidden
    final = residual + lax.psum_scatter(
        jnp.einsum(
            "nmf,mfd->nmd", selected_rows, w_down, preferred_element_type=jnp.float32
        ).astype(jnp.bfloat16),
        "mp",
        scatter_dimension=0,
        tiled=True,
    ).astype(jnp.float32)
    closing = rms_scale(final, final_gain).astype(jnp.bfloat16)
    vocab_here = w_head.shape[2]
    vocab_first = lax.axis_index(("req", "mp")) * vocab_here
    column_ids = jnp.arange(vocab_here, dtype=jnp.int32)
    logits = jnp.einsum(
        "nmd,mdv->mnv",
        lax.all_gather(closing, ("req", "mp"), axis=0, tiled=True),
        w_head,
        preferred_element_type=jnp.float32,
    )
    peak_part = jnp.max(logits, axis=-1)
    total_part = jnp.sum(jnp.exp(logits - peak_part[..., None]), axis=-1)
    wanted = targets - vocab_first
    hit_part = jnp.sum(
        jnp.where(column_ids[None, None, :] == wanted[None, :, None], logits, 0.0), axis=-1
    )

    groups = lax.axis_size("req")
    parts = lax.axis_size("mp")
    stats = jnp.stack([peak_part, total_part, hit_part])
    tenant_stats = stats.reshape(3, 2, groups, group_rows).transpose(2, 0, 1, 3)
    outgoing = jnp.broadcast_to(
        tenant_stats[:, None], (groups, parts, 3, 2, group_rows)
    ).reshape(groups * parts, 3, 2, group_rows)
    incoming = lax.all_to_all(outgoing, ("req", "mp"), 0, 0, tiled=True)
    peak_all = jnp.max(incoming[:, 0], axis=0)
    total_all = jnp.sum(incoming[:, 1] * jnp.exp(incoming[:, 0] - peak_all[None]), axis=0)
    hit_all = jnp.sum(incoming[:, 2], axis=0)
    log_likelihood = hit_all - (peak_all + jnp.log(total_all))
    gap = log_likelihood[0] - log_likelihood[1]
    group_gap = gap * response.astype(jnp.float32)
    token_out = lax.dynamic_slice_in_dim(group_gap, mp_index * own_rows, own_rows, 0)
    member_weights = member.astype(jnp.float32)
    request_sum = jnp.dot(group_gap, member_weights, precision=lax.Precision.HIGHEST)
    request_peak = jnp.max(member_weights * jnp.abs(group_gap)[:, None], axis=0)
    return (token_out, request_sum[None, :], request_peak[None, :])


def solution(mesh):
    placed = (
        P("req", None),
        P("req", None),
        P("req"),
        P(),
        P(),
        P(None, None, "mp"),
        P(),
        P(),
        P(None, "mp", None),
        P(),
        P(None, None, "mp"),
        P(None, None, "mp"),
        P(None, "mp", None),
        P(),
        P(None, None, ("req", "mp")),
    )
    return jax.shard_map(
        per_device,
        mesh=mesh,
        in_specs=placed,
        out_specs=(P(("req", "mp")), P("req", None), P("req", None)),
        check_vma=False,
    )
```

```python
import jax
import jax.numpy as jnp
from jax import lax
from jax.sharding import PartitionSpec as P

HEADS = 32
KV_HEADS = 8
HEAD_DIM = 64


epsilon = 1e-05
theta = 500000.0


def merged(part, axis, combine):
    gathered = jax.tree.map(lambda a: lax.all_gather(a, axis), part)

    def take(source):
        return jax.tree.map(lambda a: lax.dynamic_index_in_dim(a, source, 0, False), gathered)

    return lax.fori_loop(
        1, lax.axis_size(axis), lambda source, state: combine(state, take(source)), take(0)
    )


def rms_scale(entries, scaling):
    entries = entries.astype(jnp.float32)
    inverse = lax.rsqrt(jnp.mean(entries * entries, axis=-1, keepdims=True) + epsilon)
    return entries * inverse * scaling


def rotate(entries, positions):
    halfway = entries.shape[-1] // 2
    frequency = theta ** (-jnp.arange(halfway, dtype=jnp.float32) * 2.0 / entries.shape[-1])
    angles = positions.astype(jnp.float32)[:, None] * frequency[None, :]
    cosine = jnp.cos(angles)
    sine_part = jnp.sin(angles)
    former = entries[..., :halfway]
    latter = entries[..., halfway:]
    return jnp.concatenate(
        [former * cosine - latter * sine_part, latter * cosine + former * sine_part], axis=-1
    )


def request_layout(length_row, slot_count):
    end_slot = jnp.cumsum(length_row, dtype=jnp.int32)
    start_slot = end_slot - length_row
    slot_ids = jnp.arange(slot_count, dtype=jnp.int32)
    member = (slot_ids[:, None] >= start_slot[None, :]) & (slot_ids[:, None] < end_slot[None, :])
    segment = jnp.sum((slot_ids[:, None] >= end_slot[None, :]).astype(jnp.int32), axis=1)
    offset = jnp.sum(jnp.where(member, start_slot[None, :], 0), axis=1)
    return (member, segment, slot_ids - offset)


def allowed_pairs(segment):
    slot_ids = jnp.arange(segment.shape[0], dtype=jnp.int32)
    return (segment[:, None] == segment[None, :]) & (slot_ids[None, :] <= slot_ids[:, None])


def attend_heads(query, key_rows, value_rows, positions, allowed, repeat_times):
    slot_count = query.shape[1]
    query = rotate(query, positions).astype(jnp.bfloat16)
    key_rows = rotate(key_rows, positions).astype(jnp.bfloat16)
    value_rows = value_rows.astype(jnp.bfloat16)
    key_rows = jnp.repeat(key_rows, repeat_times, axis=0)
    value_rows = jnp.repeat(value_rows, repeat_times, axis=0)
    scores = jnp.einsum(
        "hqd,hkd->hqk", query, key_rows, preferred_element_type=jnp.float32
    ) * HEAD_DIM ** (-0.5)
    scores = jnp.where(allowed[None], scores, -1e30)
    highest = jnp.max(scores, axis=-1, keepdims=True)
    weights = jnp.exp(scores - highest)
    probs = (weights / jnp.sum(weights, axis=-1, keepdims=True)).astype(jnp.bfloat16)
    attended = jnp.einsum(
        "hqk,hkd->hqd", probs, value_rows, preferred_element_type=jnp.float32
    ).astype(jnp.bfloat16)
    return attended.transpose(1, 0, 2).reshape(slot_count, -1)


def per_device(
    tokens,
    lengths,
    response,
    targets,
    attn_gain,
    w_query,
    w_key,
    w_value,
    output_weight,
    mlp_gain,
    w_gate,
    w_up,
    w_down,
    final_gain,
    w_head,
):
    group_rows = tokens.shape[0]
    own_rows = group_rows // lax.axis_size("mp")
    mp_index = lax.axis_index("mp")
    member, segment, positions = request_layout(lengths[0], group_rows)
    allowed = allowed_pairs(segment)
    heads_here = w_query.shape[2] // HEAD_DIM
    sharing = HEADS // KV_HEADS
    kv_here = max(1, heads_here // sharing)
    kv_first = mp_index * heads_here // sharing * HEAD_DIM
    key_cols = lax.dynamic_slice_in_dim(w_key, kv_first, kv_here * HEAD_DIM, 2)
    value_columns = lax.dynamic_slice_in_dim(w_value, kv_first, kv_here * HEAD_DIM, 2)
    attended_list = []
    normed = rms_scale(tokens[None], attn_gain[:, None, :]).astype(jnp.bfloat16)
    width = tokens.shape[1]
    query = jnp.einsum(
        "mtd,mdhe->mhte",
        normed,
        w_query.reshape(2, width, heads_here, HEAD_DIM),
        preferred_element_type=jnp.float32,
    )
    key_value = jnp.einsum(
        "mtd,mdhe->mhte",
        normed,
        jnp.concatenate([key_cols, value_columns], axis=2).reshape(
            2, width, 2 * kv_here, HEAD_DIM
        ),
        preferred_element_type=jnp.float32,
    )
    keys_here = key_value[:, :kv_here]
    values_here = key_value[:, kv_here:]
    for model in range(2):
        attended_list.append(
            attend_heads(
                query[model],
                keys_here[model],
                values_here[model],
                positions,
                allowed,
                min(sharing, heads_here),
            )
        )
    attended = jnp.stack(attended_list, axis=1)
    selected_rows = attended
    mixed = lax.psum_scatter(
        jnp.einsum(
            "kbq,bqo->kbo", selected_rows, output_weight, preferred_element_type=jnp.float32
        ).astype(jnp.bfloat16),
        "mp",
        scatter_dimension=0,
        tiled=True,
    ).astype(jnp.float32)
    own_tokens = lax.dynamic_slice_in_dim(tokens, mp_index * own_rows, own_rows, 0)
    residual = own_tokens.astype(jnp.float32)[:, None, :] + mixed
    normed_mid = rms_scale(residual, mlp_gain).astype(jnp.bfloat16)
    row_block = lax.all_gather(normed_mid, "mp", axis=0, tiled=True)
    gate_part = jnp.einsum("nmd,mdf->nmf", row_block, w_gate, preferred_element_type=jnp.float32)
    lift_part = jnp.einsum("nmd,mdf->nmf", row_block, w_up, preferred_element_type=jnp.float32)
    hidden = (jax.nn.silu(gate_part) * lift_part).astype(jnp.bfloat16)
    selected_rows = hidden
    final = residual + lax.psum_scatter(
        jnp.einsum(
            "nmf,mfd->nmd", selected_rows, w_down, preferred_element_type=jnp.float32
        ).astype(jnp.bfloat16),
        "mp",
        scatter_dimension=0,
        tiled=True,
    ).astype(jnp.float32)
    closing = rms_scale(final, final_gain).astype(jnp.bfloat16)
    vocab_here = w_head.shape[2]
    vocab_first = lax.axis_index(("req", "mp")) * vocab_here
    column_ids = jnp.arange(vocab_here, dtype=jnp.int32)
    logits = jnp.einsum(
        "nmd,mdv->mnv",
        lax.all_gather(closing, ("req", "mp"), axis=0, tiled=True),
        w_head,
        preferred_element_type=jnp.float32,
    )
    peak_part = jnp.max(logits, axis=-1)
    total_part = jnp.sum(jnp.exp(logits - peak_part[..., None]), axis=-1)
    wanted = targets - vocab_first
    hit_part = jnp.sum(
        jnp.where(column_ids[None, None, :] == wanted[None, :, None], logits, 0.0), axis=-1
    )

    groups = lax.axis_size("req")
    parts = lax.axis_size("mp")
    stats = jnp.stack([peak_part, total_part, hit_part])
    tenant_stats = stats.reshape(3, 2, groups, group_rows).transpose(2, 0, 1, 3)
    outgoing = jnp.broadcast_to(
        tenant_stats[:, None], (groups, parts, 3, 2, group_rows)
    ).reshape(groups * parts, 3, 2, group_rows)
    incoming = lax.all_to_all(outgoing, ("req", "mp"), 0, 0, tiled=True)
    peak_all = jnp.max(incoming[:, 0], axis=0)
    total_all = jnp.sum(incoming[:, 1] * jnp.exp(incoming[:, 0] - peak_all[None]), axis=0)
    hit_all = jnp.sum(incoming[:, 2], axis=0)
    log_likelihood = hit_all - (peak_all + jnp.log(total_all))
    gap = log_likelihood[0] - log_likelihood[1]
    group_gap = gap * response.astype(jnp.float32)
    token_out = lax.dynamic_slice_in_dim(group_gap, mp_index * own_rows, own_rows, 0)
    member_weights = member.astype(jnp.float32)
    request_sum = jnp.dot(group_gap, member_weights, precision=lax.Precision.HIGHEST)
    request_peak = jnp.max(member_weights * jnp.abs(group_gap)[:, None], axis=0)
    return (token_out, request_sum[None, :], request_peak[None, :])


def solution(mesh):
    placed = (
        P("req", None),
        P("req", None),
        P("req"),
        P(),
        P(),
        P(None, None, "mp"),
        P(),
        P(),
        P(None, "mp", None),
        P(),
        P(None, None, "mp"),
        P(None, None, "mp"),
        P(None, "mp", None),
        P(),
        P(None, None, ("req", "mp")),
    )
    return jax.shard_map(
        per_device,
        mesh=mesh,
        in_specs=placed,
        out_specs=(P(("req", "mp")), P("req", None), P("req", None)),
        check_vma=False,
    )
```

```python
import jax
import jax.numpy as jnp
from jax import lax
from jax.sharding import PartitionSpec as P

HEADS = 32
KV_HEADS = 8
HEAD_DIM = 64


epsilon = 1e-05
theta = 500000.0


def merged(part, axis, combine):
    gathered = jax.tree.map(lambda a: lax.all_gather(a, axis), part)

    def take(source):
        return jax.tree.map(lambda a: lax.dynamic_index_in_dim(a, source, 0, False), gathered)

    return lax.fori_loop(
        1, lax.axis_size(axis), lambda source, state: combine(state, take(source)), take(0)
    )


def rms_scale(entries, scaling):
    entries = entries.astype(jnp.float32)
    inverse = lax.rsqrt(jnp.mean(entries * entries, axis=-1, keepdims=True) + epsilon)
    return entries * inverse * scaling


def rotate(entries, positions):
    halfway = entries.shape[-1] // 2
    frequency = theta ** (-jnp.arange(halfway, dtype=jnp.float32) * 2.0 / entries.shape[-1])
    angles = positions.astype(jnp.float32)[:, None] * frequency[None, :]
    cosine = jnp.cos(angles)
    sine_part = jnp.sin(angles)
    former = entries[..., :halfway]
    latter = entries[..., halfway:]
    return jnp.concatenate(
        [former * cosine - latter * sine_part, latter * cosine + former * sine_part], axis=-1
    )


def request_layout(length_row, slot_count):
    end_slot = jnp.cumsum(length_row, dtype=jnp.int32)
    start_slot = end_slot - length_row
    slot_ids = jnp.arange(slot_count, dtype=jnp.int32)
    member = (slot_ids[:, None] >= start_slot[None, :]) & (slot_ids[:, None] < end_slot[None, :])
    segment = jnp.sum((slot_ids[:, None] >= end_slot[None, :]).astype(jnp.int32), axis=1)
    offset = jnp.sum(jnp.where(member, start_slot[None, :], 0), axis=1)
    return (member, segment, slot_ids - offset)


def allowed_pairs(segment):
    slot_ids = jnp.arange(segment.shape[0], dtype=jnp.int32)
    return (segment[:, None] == segment[None, :]) & (slot_ids[None, :] <= slot_ids[:, None])


def attend_heads(query, key_rows, value_rows, positions, allowed, repeat_times):
    slot_count = query.shape[1]
    query = rotate(query, positions).astype(jnp.bfloat16)
    key_rows = rotate(key_rows, positions).astype(jnp.bfloat16)
    value_rows = value_rows.astype(jnp.bfloat16)
    key_rows = jnp.repeat(key_rows, repeat_times, axis=0)
    value_rows = jnp.repeat(value_rows, repeat_times, axis=0)
    scores = jnp.einsum(
        "hqd,hkd->hqk", query, key_rows, preferred_element_type=jnp.float32
    ) * HEAD_DIM ** (-0.5)
    scores = jnp.where(allowed[None], scores, -1e30)
    highest = jnp.max(scores, axis=-1, keepdims=True)
    weights = jnp.exp(scores - highest)
    probs = (weights / jnp.sum(weights, axis=-1, keepdims=True)).astype(jnp.bfloat16)
    attended = jnp.einsum(
        "hqk,hkd->hqd", probs, value_rows, preferred_element_type=jnp.float32
    ).astype(jnp.bfloat16)
    return attended.transpose(1, 0, 2).reshape(slot_count, -1)


def per_device(
    tokens,
    lengths,
    response,
    targets,
    attn_gain,
    w_query,
    w_key,
    w_value,
    output_weight,
    mlp_gain,
    w_gate,
    w_up,
    w_down,
    final_gain,
    w_head,
):
    group_rows = tokens.shape[0]
    own_rows = group_rows // lax.axis_size("mp")
    mp_index = lax.axis_index("mp")
    member, segment, positions = request_layout(lengths[0], group_rows)
    allowed = allowed_pairs(segment)
    heads_here = w_query.shape[2] // HEAD_DIM
    sharing = HEADS // KV_HEADS
    kv_here = max(1, heads_here // sharing)
    kv_first = mp_index * heads_here // sharing * HEAD_DIM
    key_cols = lax.dynamic_slice_in_dim(w_key, kv_first, kv_here * HEAD_DIM, 2)
    value_columns = lax.dynamic_slice_in_dim(w_value, kv_first, kv_here * HEAD_DIM, 2)
    attended_list = []
    normed = rms_scale(tokens[None], attn_gain[:, None, :]).astype(jnp.bfloat16)
    width = tokens.shape[1]
    query = jnp.einsum(
        "mtd,mdhe->mhte",
        normed,
        w_query.reshape(2, width, heads_here, HEAD_DIM),
        preferred_element_type=jnp.float32,
    )
    keys_here = jnp.einsum(
        "mtd,mdhe->mhte",
        normed,
        key_cols.reshape(2, width, kv_here, HEAD_DIM),
        preferred_element_type=jnp.float32,
    )
    values_here = jnp.einsum(
        "mtd,mdhe->mhte",
        normed,
        value_columns.reshape(2, width, kv_here, HEAD_DIM),
        preferred_element_type=jnp.float32,
    )
    for model in range(2):
        attended_list.append(
            attend_heads(
                query[model],
                keys_here[model],
                values_here[model],
                positions,
                allowed,
                min(sharing, heads_here),
            )
        )
    attended = jnp.stack(attended_list, axis=1)
    selected_rows = attended
    mixed = lax.psum_scatter(
        jnp.einsum(
            "kbq,bqo->kbo", selected_rows, output_weight, preferred_element_type=jnp.float32
        ).astype(jnp.bfloat16),
        "mp",
        scatter_dimension=0,
        tiled=True,
    ).astype(jnp.float32)
    own_tokens = lax.dynamic_slice_in_dim(tokens, mp_index * own_rows, own_rows, 0)
    residual = own_tokens.astype(jnp.float32)[:, None, :] + mixed
    normed_mid = rms_scale(residual, mlp_gain).astype(jnp.bfloat16)
    row_block = lax.all_gather(normed_mid, "mp", axis=0, tiled=True)
    gate_part = jnp.einsum("nmd,mdf->nmf", row_block, w_gate, preferred_element_type=jnp.float32)
    lift_part = jnp.einsum("nmd,mdf->nmf", row_block, w_up, preferred_element_type=jnp.float32)
    hidden = (jax.nn.silu(gate_part) * lift_part).astype(jnp.bfloat16)
    selected_rows = hidden
    final = residual + lax.psum_scatter(
        jnp.einsum(
            "nmf,mfd->nmd", selected_rows, w_down, preferred_element_type=jnp.float32
        ).astype(jnp.bfloat16),
        "mp",
        scatter_dimension=0,
        tiled=True,
    ).astype(jnp.float32)
    closing = rms_scale(final, final_gain).astype(jnp.bfloat16)
    vocab_here = w_head.shape[2]
    vocab_first = lax.axis_index(("req", "mp")) * vocab_here
    column_ids = jnp.arange(vocab_here, dtype=jnp.int32)
    logits = jnp.einsum(
        "nmd,mdv->mnv",
        lax.all_gather(closing, ("mp", "req"), axis=0, tiled=True),
        w_head,
        preferred_element_type=jnp.float32,
    )
    peak_part = jnp.max(logits, axis=-1)
    total_part = jnp.sum(jnp.exp(logits - peak_part[..., None]), axis=-1)
    gathered_targets = targets.reshape(
        lax.axis_size("req"), lax.axis_size("mp"), own_rows
    ).transpose(1, 0, 2).reshape(-1)
    wanted = gathered_targets - vocab_first
    hit_part = jnp.sum(
        jnp.where(column_ids[None, None, :] == wanted[None, :, None], logits, 0.0), axis=-1
    )

    groups = lax.axis_size("req")
    parts = lax.axis_size("mp")
    stats = jnp.stack([peak_part, total_part, hit_part])
    tenant_stats = (
        stats.reshape(3, 2, parts, groups, own_rows)
        .transpose(3, 0, 1, 2, 4)
        .reshape(groups, 3, 2, group_rows)
    )
    outgoing = jnp.broadcast_to(
        tenant_stats[:, None], (groups, parts, 3, 2, group_rows)
    ).reshape(groups * parts, 3, 2, group_rows)
    incoming = lax.all_to_all(outgoing, ("req", "mp"), 0, 0, tiled=True)
    peak_all = jnp.max(incoming[:, 0], axis=0)
    total_all = jnp.sum(incoming[:, 1] * jnp.exp(incoming[:, 0] - peak_all[None]), axis=0)
    hit_all = jnp.sum(incoming[:, 2], axis=0)
    log_likelihood = hit_all - (peak_all + jnp.log(total_all))
    gap = log_likelihood[0] - log_likelihood[1]
    group_gap = gap * response.astype(jnp.float32)
    token_out = lax.dynamic_slice_in_dim(group_gap, mp_index * own_rows, own_rows, 0)
    member_weights = member.astype(jnp.float32)
    request_sum = jnp.dot(group_gap, member_weights, precision=lax.Precision.HIGHEST)
    request_peak = jnp.max(member_weights * jnp.abs(group_gap)[:, None], axis=0)
    return (token_out, request_sum[None, :], request_peak[None, :])


def solution(mesh):
    placed = (
        P("req", None),
        P("req", None),
        P("req"),
        P(),
        P(),
        P(None, None, "mp"),
        P(),
        P(),
        P(None, "mp", None),
        P(),
        P(None, None, "mp"),
        P(None, None, "mp"),
        P(None, "mp", None),
        P(),
        P(None, None, ("req", "mp")),
    )
    return jax.shard_map(
        per_device,
        mesh=mesh,
        in_specs=placed,
        out_specs=(P(("req", "mp")), P("req", None), P("req", None)),
        check_vma=False,
    )
```
